32 devices in a mesh: parts: 2 (over y), tm: 4 (over x, core), cols: 4 (over z).
Axes of the slice: x: 2, y: 2, z: 4, core: 2. Of those that a mesh axis runs over, the one named last changes fastest.
Arguments:
- noise: float32 [16, 1024, 1024], P(('parts', 'tm'), None, 'cols'), parts along dimension 0, may hold values from -6 to 6
- inv_diag: float32 [16, 1024, 1024], P(('parts', 'tm'), None, 'cols'), parts along dimension 0, may hold values from -2 to 2, as said below
- coupling: float32 [16, 1024, 1024], P(('parts', 'tm'), None, 'cols'), parts along dimension 0, may hold values from -1 to 1, as said below
- order: int32 [1024], replicated, may hold values from 0 to 1023, each once
Outputs:
- sample: float32 [16, 1024, 1024], P(('parts', 'tm'), None, 'cols'), parts along dimension 0
The draws below stay inside these ranges and needn't reach their ends.
There are 2 independent parts, one for each index of `parts`. The reference program is written for one: setup_inputs(seed, part) draws one part's arguments, and reference() takes and returns one part's arrays. A program takes and returns all parts, laid end to end along the dimension named above; an argument that names none is the same for every part. Nothing has to cross between parts.
Inputs may be any that keep to these rules, and one draw needn't show every extreme that they name: `order`: each of 0 to 1023 appears once. `inv_diag`: diagonal entries lie between 0.5 and 2, off-diagonal entries are small in magnitude. `coupling`: diagonal entries lie between 0.5 and 0.97, off-diagonal entries are small in magnitude.
All inputs are finite; a program needn't handle non-finite values.
Results may differ from the reference program's by a relative error of at most 0.00013.
Values sent between devices are 32-bit elements; how exact they have to be, the bound alone decides.
No kernel may reach another device: no remote copies, remote signals or barrier semaphores. Data moves between devices by JAX's collectives and lax.ppermute only.
A program may use at most 128 MiB of HBM per device.

```python
import math
import jax
import jax.numpy as jnp
from jax import lax

M = 1024
NT = 8
S = 1024


def draw_inv_diag(key, part):
    key_diag = jax.random.fold_in(key, 11)
    key_off = jax.random.fold_in(key, 12)
    diagonal_mask = jnp.arange(M)[:, None] == jnp.arange(M)[None, :]
    diag_values = jnp.exp(jax.random.uniform(key_diag, (NT, M, 1), minval=math.log(0.5), maxval=math.log(2.0)))
    off_values = jax.random.normal(key_off, (NT, M, M)) * (0.3 / math.sqrt(M))
    return jnp.where(diagonal_mask[None, :, :], diag_values, off_values).astype(jnp.float32)


def draw_coupling(key, part):
    key_rate = jax.random.fold_in(key, 21)
    key_off = jax.random.fold_in(key, 22)
    diagonal_mask = jnp.arange(M)[:, None] == jnp.arange(M)[None, :]
    rates = jax.random.uniform(key_rate, (NT, M, 1), minval=0.5, maxval=0.97)
    off_values = jax.random.normal(key_off, (NT, M, M)) * (0.25 / math.sqrt(M))
    return jnp.where(diagonal_mask[None, :, :], rates, off_values).astype(jnp.float32)


def block_levels(key, shape, split, least, top_value):
    def one(axis_at, shards_of):
        steps = jax.random.uniform(jax.random.fold_in(jax.random.fold_in(key, 6), axis_at), (shards_of,), jnp.float32, least / len(split), top_value / len(split))
        return jnp.repeat(jnp.exp(steps), shape[axis_at] // shards_of).reshape((-1,) + (1,) * (len(shape) - axis_at - 1))

    factor_of = one(*split[0])
    for cut in split[1:]:
        factor_of = factor_of * one(*cut)
    return factor_of


def normal_values(stream_key, shape, scale, bound, cuts=(), kind=jnp.bfloat16):
    loudness = block_levels(stream_key, shape, cuts, -0.22, 0.18) if cuts else 1.0
    result = jax.random.normal(stream_key, shape, jnp.float32) * scale * loudness
    return jnp.minimum(jnp.maximum(result, -bound), bound).astype(kind)


def setup_inputs(seed: int = 0, part: int = 0) -> dict:
    key_list = jax.random.split(jax.random.key(seed), 5)
    own_keys = jax.random.split(jax.random.fold_in(key_list[4], part), 5)
    noise = normal_values(own_keys[0], (NT, M, S), 1.0, 6.0, ((0, 4), (2, 4)), jnp.float32)
    inv_diag = draw_inv_diag(jax.random.fold_in(jax.random.fold_in(key_list[4], part), 71), part)
    coupling = draw_coupling(jax.random.fold_in(jax.random.fold_in(key_list[4], part), 71), part)
    order = jax.random.permutation(key_list[3], M).astype(jnp.int32)
    return {"noise": noise, "inv_diag": inv_diag, "coupling": coupling, "order": order}


def reference(noise, inv_diag, coupling, order):
    precise = lax.Precision.HIGHEST
    driven = jnp.einsum("tmn,tns->tms", inv_diag, noise, precision=precise, preferred_element_type=jnp.float32)

    def back_step(carried, inputs):
        driven_block, coupling_block = inputs
        updated = driven_block + jnp.dot(coupling_block, carried, precision=precise, preferred_element_type=jnp.float32)
        return updated, updated

    initial = jnp.zeros((noise.shape[1], noise.shape[2]), jnp.float32)
    _, field = lax.scan(back_step, initial, (driven, coupling), reverse=True)
    return jnp.take(field, order.astype(jnp.int32), axis=1)
```

```python
import jax
import jax.numpy as jnp
from jax import lax
from jax.sharding import PartitionSpec as P

precise = lax.Precision.HIGHEST


def shifted(block, axis, distance):
    devices = range(lax.axis_size(axis))
    route = [(i - distance, i) for i in devices if i - distance in devices]
    return lax.ppermute(block, axis, route)


def apply(matrix, operand):
    return jnp.dot(matrix, operand, precision=precise, preferred_element_type=jnp.float32)


def shards(noise, inv_diag, coupling, order):
    block_count = noise.shape[0]
    inv_full = lax.all_gather(inv_diag, "cols", axis=2, tiled=True)
    coupling_full = lax.all_gather(coupling, "cols", axis=2, tiled=True)
    driven = jnp.einsum(
        "kmn,kns->kms", inv_full, noise, precision=precise, preferred_element_type=jnp.float32
    )

    def chain(entering):
        carried = entering
        results = [None] * block_count
        for block in range(block_count - 1, -1, -1):
            carried = driven[block] + apply(coupling_full[block], carried)
            results[block] = carried
        return results

    def relay_step(step, entering):
        return shifted(chain(entering)[0], "tm", -1)

    entering = lax.fori_loop(0, lax.axis_size("tm") - 1, relay_step, jnp.zeros_like(driven[0]))
    stacked = jnp.stack(chain(entering), axis=0)
    return jnp.take(stacked, order, axis=1)


def solution(mesh):
    return jax.shard_map(
        shards,
        mesh=mesh,
        in_specs=(
            P(("parts", "tm"), None, "cols"),
            P(("parts", "tm"), None, "cols"),
            P(("parts", "tm"), None, "cols"),
            P(),
        ),
        out_specs=P(("parts", "tm"), None, "cols"),
        check_vma=False,
    )
```

```python
import jax
import jax.numpy as jnp
from jax import lax
from jax.sharding import PartitionSpec as P

fast = lax.Precision.HIGH


def shifted(block, axis, distance):
    devices = range(lax.axis_size(axis))
    route = [(i - distance, i) for i in devices if i - distance in devices]
    return lax.ppermute(block, axis, route)


def apply(matrix, operand):
    return jnp.dot(matrix, operand, precision=fast, preferred_element_type=jnp.float32)


def shards(noise, inv_diag, coupling, order):
    block_count = noise.shape[0]
    sample_count = noise.shape[2]
    pieces = 2 if sample_count % 256 == 0 else 1
    width = sample_count // pieces
    inv_full = lax.all_gather(inv_diag, "cols", axis=2, tiled=True)
    coupling_full = [
        lax.all_gather(coupling[block], "cols", axis=1, tiled=True) for block in range(block_count)
    ]
    driven = jnp.einsum(
        "kmn,kns->kms", inv_full, noise, precision=fast, preferred_element_type=jnp.float32
    )
    driven_pieces = [
        [driven[block][:, p * width:(p + 1) * width] for p in range(pieces)]
        for block in range(block_count)
    ]

    def chain(entering, piece, skip_last):
        carried = entering
        results = [None] * block_count
        for block in range(block_count - 1, -1, -1):
            if skip_last and block == block_count - 1:
                carried = driven_pieces[block][piece]
            else:
                carried = driven_pieces[block][piece] + apply(coupling_full[block], carried)
            results[block] = carried
        return results

    first = [shifted(chain(None, p, True)[0], "tm", -1) for p in range(pieces)]

    def relay_step(step, entering):
        return [shifted(chain(entering[p], p, False)[0], "tm", -1) for p in range(pieces)]

    entering = lax.fori_loop(0, lax.axis_size("tm") - 2, relay_step, first)
    finals = [chain(entering[p], p, False) for p in range(pieces)]
    stacked = jnp.stack(
        [jnp.concatenate([finals[p][block] for p in range(pieces)], axis=1) for block in range(block_count)],
        axis=0,
    )
    return stacked.at[:, order].get(mode="promise_in_bounds")


def solution(mesh):
    return jax.shard_map(
        shards,
        mesh=mesh,
        in_specs=(
            P(("parts", "tm"), None, "cols"),
            P(("parts", "tm"), None, "cols"),
            P(("parts", "tm"), None, "cols"),
            P(),
        ),
        out_specs=P(("parts", "tm"), None, "cols"),
        check_vma=False,
    )
```

```python
import jax
import jax.numpy as jnp
from jax import lax
from jax.sharding import PartitionSpec as P

low = jnp.bfloat16


def shifted(block, axis, distance):
    devices = range(lax.axis_size(axis))
    route = [(i - distance, i) for i in devices if i - distance in devices]
    return lax.ppermute(block, axis, route)


def split(value, count):
    parts = []
    rest = value
    for index in range(count):
        kept = lax.reduce_precision(rest, exponent_bits=8, mantissa_bits=7)
        parts.append(kept.astype(low))
        if index < count - 1:
            rest = rest - kept
    return parts


def bdot(left, right):
    return jnp.dot(left, right, preferred_element_type=jnp.float32)


def apply(matrix_parts, operand):
    high, small = matrix_parts
    operand_high, operand_small = split(operand, 2)
    return bdot(high, operand_high) + (bdot(high, operand_small) + bdot(small, operand_high))


def shards(noise, inv_diag, coupling, order):
    block_count = noise.shape[0]
    node_count = noise.shape[1]
    sample_count = noise.shape[2]
    pieces = 2 if sample_count % 256 == 0 else 1
    width = sample_count // pieces
    inv_full = lax.all_gather(inv_diag, "cols", axis=2, tiled=True)
    coupling_parts = [
        split(lax.all_gather(coupling[block], "cols", axis=1, tiled=True), 2)
        for block in range(block_count)
    ]
    driven = [apply(split(inv_full[block], 2), noise[block]) for block in range(block_count)]
    driven_pieces = [
        [driven[block][:, p * width:(p + 1) * width] for p in range(pieces)]
        for block in range(block_count)
    ]

    def chain(entering, piece, skip_last):
        carried = entering
        results = [None] * block_count
        for block in range(block_count - 1, -1, -1):
            if skip_last and block == block_count - 1:
                carried = driven_pieces[block][piece]
            else:
                carried = driven_pieces[block][piece] + apply(coupling_parts[block], carried)
            results[block] = carried
        return results

    first = [shifted(chain(None, p, True)[0], "tm", -1) for p in range(pieces)]

    def relay_step(step, entering):
        return [shifted(chain(entering[p], p, False)[0], "tm", -1) for p in range(pieces)]

    entering = lax.fori_loop(0, lax.axis_size("tm") - 2, relay_step, first)
    finals = [chain(entering[p], p, False) for p in range(pieces)]
    selector = (order[:, None] == jnp.arange(node_count, dtype=order.dtype)[None, :]).astype(low)
    outputs = []
    for block in range(block_count):
        field = jnp.concatenate([finals[p][block] for p in range(pieces)], axis=1)
        top, middle, bottom = split(field, 3)
        outputs.append(bdot(selector, top) + (bdot(selector, middle) + bdot(selector, bottom)))
    return jnp.stack(outputs, axis=0)


def solution(mesh):
    return jax.shard_map(
        shards,
        mesh=mesh,
        in_specs=(
            P(("parts", "tm"), None, "cols"),
            P(("parts", "tm"), None, "cols"),
            P(("parts", "tm"), None, "cols"),
            P(),
        ),
        out_specs=P(("parts", "tm"), None, "cols"),
        check_vma=False,
    )
```

```python
import jax
import jax.numpy as jnp
from jax import lax
from jax.sharding import PartitionSpec as P

low = jnp.bfloat16


def shifted(block, axis, distance):
    devices = range(lax.axis_size(axis))
    route = [(i - distance, i) for i in devices if i - distance in devices]
    return lax.ppermute(block, axis, route)


def split(value, count):
    parts = []
    rest = value
    for index in range(count):
        kept = lax.reduce_precision(rest, exponent_bits=8, mantissa_bits=7)
        parts.append(kept.astype(low))
        if index < count - 1:
            rest = rest - kept
    return parts


def bdot(left, right):
    return jnp.dot(left, right, preferred_element_type=jnp.float32)


def apply(matrix_parts, operand):
    high, small = matrix_parts
    width = operand.shape[1]
    operand_high, operand_small = split(operand, 2)
    both = bdot(high, jnp.concatenate([operand_high, operand_small], axis=1))
    return both[:, :width] + (both[:, width:] + bdot(small, operand_high))


def gathered(tile, after):
    tile, _ = lax.optimization_barrier((tile, after))
    return lax.all_gather(tile, "cols", axis=tile.ndim - 1, tiled=True)


def shards(noise, inv_diag, coupling, order):
    block_count = noise.shape[0]
    node_count = noise.shape[1]
    sample_count = noise.shape[2]
    inv_full = lax.all_gather(inv_diag, "cols", axis=2, tiled=True)
    coupling_parts = []
    previous = inv_full
    for block in range(block_count):
        previous = gathered(coupling[block], previous)
        coupling_parts.append(split(previous, 2))
    driven = [apply(split(inv_full[block], 2), noise[block]) for block in range(block_count)]

    def chain(entering, skip_last):
        carried = entering
        results = [None] * block_count
        for block in range(block_count - 1, -1, -1):
            if skip_last and block == block_count - 1:
                carried = driven[block]
            else:
                carried = driven[block] + apply(coupling_parts[block], carried)
            results[block] = carried
        return results

    first = shifted(chain(None, True)[0], "tm", -1)

    def relay_step(step, entering):
        return shifted(chain(entering, False)[0], "tm", -1)

    entering = lax.fori_loop(0, lax.axis_size("tm") - 2, relay_step, first)
    finals = chain(entering, False)
    selector = (order[:, None] == jnp.arange(node_count, dtype=order.dtype)[None, :]).astype(low)
    outputs = []
    for block in range(block_count):
        picked = bdot(selector, jnp.concatenate(split(finals[block], 3), axis=1))
        top = picked[:, :sample_count]
        middle = picked[:, sample_count:2 * sample_count]
        bottom = picked[:, 2 * sample_count:]
        outputs.append(top + (middle + bottom))
    return jnp.stack(outputs, axis=0)


def solution(mesh):
    return jax.shard_map(
        shards,
        mesh=mesh,
        in_specs=(
            P(("parts", "tm"), None, "cols"),
            P(("parts", "tm"), None, "cols"),
            P(("parts", "tm"), None, "cols"),
            P(),
        ),
        out_specs=P(("parts", "tm"), None, "cols"),
        check_vma=False,
    )
```

```python
import jax
import jax.numpy as jnp
from jax import lax
from jax.sharding import PartitionSpec as P

low = jnp.bfloat16


def shifted(block, axis, distance):
    devices = range(lax.axis_size(axis))
    route = [(i - distance, i) for i in devices if i - distance in devices]
    return lax.ppermute(block, axis, route)


def split(value, count):
    parts = []
    rest = value
    for index in range(count):
        kept = lax.reduce_precision(rest, exponent_bits=8, mantissa_bits=7)
        parts.append(kept.astype(low))
        if index < count - 1:
            rest = rest - kept
    return parts


def bdot(left, right):
    return jnp.dot(left, right, preferred_element_type=jnp.float32)


def apply(matrix_parts, operand):
    high, small = matrix_parts
    width = operand.shape[1]
    operand_high, operand_small = split(operand, 2)
    both = bdot(high, jnp.concatenate([operand_high, operand_small], axis=1))
    return both[:, :width] + (both[:, width:] + bdot(small, operand_high))


def line_reduce_scatter(partial, axis):
    count = lax.axis_size(axis)
    me = lax.axis_index(axis)
    width = partial.shape[2] // count

    def tile(owner):
        owner = jnp.clip(owner, 0, count - 1)
        return lax.dynamic_slice_in_dim(partial, owner * width, width, axis=2)

    rightward = jnp.zeros_like(tile(me))
    leftward = jnp.zeros_like(tile(me))
    for step in range(1, count):
        right_route = [(k, k + 1) for k in range(0, min(step, count - 1))]
        left_route = [(k, k - 1) for k in range(max(count - step, 1), count)]
        rightward = lax.ppermute(tile(me + count - step) + rightward, axis, right_route)
        leftward = lax.ppermute(tile(me - count + step) + leftward, axis, left_route)
    return tile(me) + (rightward + leftward)


def shards(noise, inv_diag, coupling, order):
    block_count = noise.shape[0]
    node_count = noise.shape[1]
    sample_count = noise.shape[2]
    coupling_full = lax.all_gather(coupling, "cols", axis=2, tiled=True)
    noise_rows = lax.all_to_all(noise, "cols", 1, 2, tiled=True)
    partial = jnp.stack(
        [apply(split(inv_diag[block], 2), noise_rows[block]) for block in range(block_count)], axis=0
    )
    driven_all = line_reduce_scatter(partial, "cols")
    driven = [driven_all[block] for block in range(block_count)]
    coupling_parts = [split(coupling_full[block], 2) for block in range(block_count)]

    def chain(entering, skip_last):
        carried = entering
        results = [None] * block_count
        for block in range(block_count - 1, -1, -1):
            if skip_last and block == block_count - 1:
                carried = driven[block]
            else:
                carried = driven[block] + apply(coupling_parts[block], carried)
            results[block] = carried
        return results

    first = shifted(chain(None, True)[0], "tm", -1)

    def relay_step(step, entering):
        return shifted(chain(entering, False)[0], "tm", -1)

    entering = lax.fori_loop(0, lax.axis_size("tm") - 2, relay_step, first)
    finals = chain(entering, False)
    selector = (order[:, None] == jnp.arange(node_count, dtype=order.dtype)[None, :]).astype(low)
    outputs = []
    for block in range(block_count):
        picked = bdot(selector, jnp.concatenate(split(finals[block], 3), axis=1))
        top = picked[:, :sample_count]
        middle = picked[:, sample_count:2 * sample_count]
        bottom = picked[:, 2 * sample_count:]
        outputs.append(top + (middle + bottom))
    return jnp.stack(outputs, axis=0)


def solution(mesh):
    return jax.shard_map(
        shards,
        mesh=mesh,
        in_specs=(
            P(("parts", "tm"), None, "cols"),
            P(("parts", "tm"), None, "cols"),
            P(("parts", "tm"), None, "cols"),
            P(),
        ),
        out_specs=P(("parts", "tm"), None, "cols"),
        check_vma=False,
    )
```

```python
import jax
import jax.numpy as jnp
from jax import lax
from jax.sharding import PartitionSpec as P

low = jnp.bfloat16


def shifted(block, axis, distance):
    devices = range(lax.axis_size(axis))
    route = [(i - distance, i) for i in devices if i - distance in devices]
    return lax.ppermute(block, axis, route)


def split(value, count):
    parts = []
    rest = value
    for index in range(count):
        kept = lax.reduce_precision(rest, exponent_bits=8, mantissa_bits=7)
        parts.append(kept.astype(low))
        if index < count - 1:
            rest = rest - kept
    return parts


def bdot(left, right):
    return jnp.dot(left, right, preferred_element_type=jnp.float32)


def apply(matrix_parts, operand):
    high, small = matrix_parts
    width = operand.shape[1]
    operand_high, operand_small = split(operand, 2)
    both = bdot(high, jnp.concatenate([operand_high, operand_small], axis=1))
    return both[:, :width] + (both[:, width:] + bdot(small, operand_high))


def line_reduce_scatter(partial, axis):
    count = lax.axis_size(axis)
    me = lax.axis_index(axis)
    width = partial.shape[2] // count

    def tile(owner):
        owner = jnp.clip(owner, 0, count - 1)
        return lax.dynamic_slice_in_dim(partial, owner * width, width, axis=2)

    rightward = jnp.zeros_like(tile(me))
    leftward = jnp.zeros_like(tile(me))
    for step in range(1, count):
        right_route = [(k, k + 1) for k in range(0, min(step, count - 1))]
        left_route = [(k, k - 1) for k in range(max(count - step, 1), count)]
        rightward = lax.ppermute(tile(me + count - step) + rightward, axis, right_route)
        leftward = lax.ppermute(tile(me - count + step) + leftward, axis, left_route)
    return tile(me) + (rightward + leftward)


def add_at(whole, piece, slot, axis):
    count = whole.shape[axis] // piece.shape[axis]
    start = jnp.clip(slot, 0, count - 1) * piece.shape[axis]
    current = lax.dynamic_slice_in_dim(whole, start, piece.shape[axis], axis=axis)
    return lax.dynamic_update_slice_in_dim(whole, current + piece, start, axis=axis)


def line_all_gather(tile, axis):
    count = lax.axis_size(axis)
    me = lax.axis_index(axis)
    last = tile.ndim - 1
    shape = tile.shape[:-1] + (count * tile.shape[-1],)
    whole = add_at(jnp.zeros(shape, tile.dtype), tile, me, last)
    from_left = tile
    from_right = tile
    for step in range(1, count):
        from_left = lax.ppermute(from_left, axis, [(k, k + 1) for k in range(step - 1, count - 1)])
        from_right = lax.ppermute(from_right, axis, [(k, k - 1) for k in range(1, count - step + 1)])
        whole = add_at(whole, from_left, me - step, last)
        whole = add_at(whole, from_right, me + step, last)
    return whole


def line_all_to_all(value, axis):
    count = lax.axis_size(axis)
    me = lax.axis_index(axis)
    rows = value.shape[1] // count

    def own_rows(target):
        return lax.dynamic_slice_in_dim(value, jnp.clip(target, 0, count - 1) * rows, rows, axis=1)

    shape = (value.shape[0], rows, count * value.shape[2])
    whole = add_at(jnp.zeros(shape, value.dtype), own_rows(me), me, 2)
    for distance in range(1, count):
        right = lax.ppermute(own_rows(me + distance), axis, [(k, k + distance) for k in range(0, count - distance)])
        left = lax.ppermute(own_rows(me - distance), axis, [(k, k - distance) for k in range(distance, count)])
        whole = add_at(whole, right, me - distance, 2)
        whole = add_at(whole, left, me + distance, 2)
    return whole


def shards(noise, inv_diag, coupling, order):
    block_count = noise.shape[0]
    node_count = noise.shape[1]
    sample_count = noise.shape[2]
    coupling_full = line_all_gather(coupling, "cols")
    noise_rows = line_all_to_all(noise, "cols")
    partial = jnp.stack(
        [apply(split(inv_diag[block], 2), noise_rows[block]) for block in range(block_count)], axis=0
    )
    driven_all = line_reduce_scatter(partial, "cols")
    driven = [driven_all[block] for block in range(block_count)]
    coupling_parts = [split(coupling_full[block], 2) for block in range(block_count)]

    def chain(entering, skip_last):
        carried = entering
        results = [None] * block_count
        for block in range(block_count - 1, -1, -1):
            if skip_last and block == block_count - 1:
                carried = driven[block]
            else:
                carried = driven[block] + apply(coupling_parts[block], carried)
            results[block] = carried
        return results

    first = shifted(chain(None, True)[0], "tm", -1)

    def relay_step(step, entering):
        return shifted(chain(entering, False)[0], "tm", -1)

    entering = lax.fori_loop(0, lax.axis_size("tm") - 2, relay_step, first)
    finals = chain(entering, False)
    selector = (order[:, None] == jnp.arange(node_count, dtype=order.dtype)[None, :]).astype(low)
    outputs = []
    for block in range(block_count):
        picked = bdot(selector, jnp.concatenate(split(finals[block], 3), axis=1))
        top = picked[:, :sample_count]
        middle = picked[:, sample_count:2 * sample_count]
        bottom = picked[:, 2 * sample_count:]
        outputs.append(top + (middle + bottom))
    return jnp.stack(outputs, axis=0)


def solution(mesh):
    return jax.shard_map(
        shards,
        mesh=mesh,
        in_specs=(
            P(("parts", "tm"), None, "cols"),
            P(("parts", "tm"), None, "cols"),
            P(("parts", "tm"), None, "cols"),
            P(),
        ),
        out_specs=P(("parts", "tm"), None, "cols"),
        check_vma=False,
    )
```

```python
import jax
import jax.numpy as jnp
from jax import lax
from jax.sharding import PartitionSpec as P

low = jnp.bfloat16


def shifted(block, axis, distance):
    devices = range(lax.axis_size(axis))
    route = [(i - distance, i) for i in devices if i - distance in devices]
    return lax.ppermute(block, axis, route)


def split(value, count):
    parts = []
    rest = value
    for index in range(count):
        kept = lax.reduce_precision(rest, exponent_bits=8, mantissa_bits=7)
        parts.append(kept.astype(low))
        if index < count - 1:
            rest = rest - kept
    return parts


def bdot(left, right):
    return jnp.dot(left, right, preferred_element_type=jnp.float32)


def apply(matrix_parts, operand):
    high, small = matrix_parts
    width = operand.shape[1]
    operand_high, operand_small = split(operand, 2)
    both = bdot(high, jnp.concatenate([operand_high, operand_small], axis=1))
    return both[:, :width] + (both[:, width:] + bdot(small, operand_high))


def line_reduce_scatter(partial, axis):
    count = lax.axis_size(axis)
    me = lax.axis_index(axis)
    width = partial.shape[2] // count

    def tile(owner):
        owner = jnp.clip(owner, 0, count - 1)
        return lax.dynamic_slice_in_dim(partial, owner * width, width, axis=2)

    rightward = jnp.zeros_like(tile(me))
    leftward = jnp.zeros_like(tile(me))
    for step in range(1, count):
        right_route = [(k, k + 1) for k in range(0, min(step, count - 1))]
        left_route = [(k, k - 1) for k in range(max(count - step, 1), count)]
        rightward = lax.ppermute(tile(me + count - step) + rightward, axis, right_route)
        leftward = lax.ppermute(tile(me - count + step) + leftward, axis, left_route)
    return tile(me) + (rightward + leftward)


def add_at(whole, piece, slot, axis):
    count = whole.shape[axis] // piece.shape[axis]
    start = jnp.clip(slot, 0, count - 1) * piece.shape[axis]
    current = lax.dynamic_slice_in_dim(whole, start, piece.shape[axis], axis=axis)
    return lax.dynamic_update_slice_in_dim(whole, current + piece, start, axis=axis)


def line_all_gather(tile, axis):
    count = lax.axis_size(axis)
    me = lax.axis_index(axis)
    last = tile.ndim - 1
    shape = tile.shape[:-1] + (count * tile.shape[-1],)
    whole = add_at(jnp.zeros(shape, tile.dtype), tile, me, last)
    from_left = tile
    from_right = tile
    for step in range(1, count):
        from_left = lax.ppermute(from_left, axis, [(k, k + 1) for k in range(step - 1, count - 1)])
        from_right = lax.ppermute(from_right, axis, [(k, k - 1) for k in range(1, count - step + 1)])
        whole = add_at(whole, from_left, me - step, last)
        whole = add_at(whole, from_right, me + step, last)
    return whole


def line_all_to_all(value, axis):
    count = lax.axis_size(axis)
    me = lax.axis_index(axis)
    rows = value.shape[1] // count

    def own_rows(target):
        return lax.dynamic_slice_in_dim(value, jnp.clip(target, 0, count - 1) * rows, rows, axis=1)

    shape = (value.shape[0], rows, count * value.shape[2])
    whole = add_at(jnp.zeros(shape, value.dtype), own_rows(me), me, 2)
    for distance in range(1, count):
        right = lax.ppermute(own_rows(me + distance), axis, [(k, k + distance) for k in range(0, count - distance)])
        left = lax.ppermute(own_rows(me - distance), axis, [(k, k - distance) for k in range(distance, count)])
        whole = add_at(whole, right, me - distance, 2)
        whole = add_at(whole, left, me + distance, 2)
    return whole


def shards(noise, inv_diag, coupling, order):
    block_count = noise.shape[0]
    node_count = noise.shape[1]
    sample_count = noise.shape[2]
    coupling_full = line_all_gather(coupling, "cols")
    noise_rows = line_all_to_all(noise, "cols")
    partial = jnp.stack(
        [apply(split(inv_diag[block], 2), noise_rows[block]) for block in range(block_count)], axis=0
    )
    driven_all = line_reduce_scatter(partial, "cols")
    driven = [driven_all[block] for block in range(block_count)]
    coupling_parts = [split(coupling_full[block], 2) for block in range(block_count)]

    def chain(entering, skip_last):
        carried = entering
        results = [None] * block_count
        for block in range(block_count - 1, -1, -1):
            if skip_last and block == block_count - 1:
                carried = driven[block]
            else:
                carried = driven[block] + apply(coupling_parts[block], carried)
            results[block] = carried
        return results

    relays = lax.axis_size("tm")
    entering = jnp.zeros_like(driven[0])
    for step in range(relays - 1):
        sender = relays - 1 - step
        leaving = chain(entering, step == 0)[0]
        entering = entering + lax.ppermute(leaving, "tm", [(sender, sender - 1)])
    finals = chain(entering, False)
    selector = (order[:, None] == jnp.arange(node_count, dtype=order.dtype)[None, :]).astype(low)
    pieces = [part for block in range(block_count) for part in split(finals[block], 3)]
    picked = bdot(selector, jnp.concatenate(pieces, axis=1))
    outputs = []
    for block in range(block_count):
        base = 3 * block * sample_count
        top = picked[:, base:base + sample_count]
        middle = picked[:, base + sample_count:base + 2 * sample_count]
        bottom = picked[:, base + 2 * sample_count:base + 3 * sample_count]
        outputs.append(top + (middle + bottom))
    return jnp.stack(outputs, axis=0)


def solution(mesh):
    return jax.shard_map(
        shards,
        mesh=mesh,
        in_specs=(
            P(("parts", "tm"), None, "cols"),
            P(("parts", "tm"), None, "cols"),
            P(("parts", "tm"), None, "cols"),
            P(),
        ),
        out_specs=P(("parts", "tm"), None, "cols"),
        check_vma=False,
    )
```

```python
import jax
import jax.numpy as jnp
from jax import lax
from jax.sharding import PartitionSpec as P

low = jnp.bfloat16


def shifted(block, axis, distance):
    devices = range(lax.axis_size(axis))
    route = [(i - distance, i) for i in devices if i - distance in devices]
    return lax.ppermute(block, axis, route)


def split(value, count):
    parts = []
    rest = value
    for index in range(count):
        kept = lax.reduce_precision(rest, exponent_bits=8, mantissa_bits=7)
        parts.append(kept.astype(low))
        if index < count - 1:
            rest = rest - kept
    return parts


def bdot(left, right):
    return jnp.dot(left, right, preferred_element_type=jnp.float32)


def apply(matrix_parts, operand):
    high, small = matrix_parts
    width = operand.shape[1]
    operand_high, operand_small = split(operand, 2)
    both = bdot(high, jnp.concatenate([operand_high, operand_small], axis=1))
    return both[:, :width] + (both[:, width:] + bdot(small, operand_high))


def add_at(whole, piece, slot, axis):
    count = whole.shape[axis] // piece.shape[axis]
    start = jnp.clip(slot, 0, count - 1) * piece.shape[axis]
    current = lax.dynamic_slice_in_dim(whole, start, piece.shape[axis], axis=axis)
    return lax.dynamic_update_slice_in_dim(whole, current + piece, start, axis=axis)


def line_all_gather(tile, axis):
    count = lax.axis_size(axis)
    me = lax.axis_index(axis)
    last = tile.ndim - 1
    shape = tile.shape[:-1] + (count * tile.shape[-1],)
    whole = add_at(jnp.zeros(shape, tile.dtype), tile, me, last)
    from_left = tile
    from_right = tile
    for step in range(1, count):
        from_left = lax.ppermute(from_left, axis, [(k, k + 1) for k in range(step - 1, count - 1)])
        from_right = lax.ppermute(from_right, axis, [(k, k - 1) for k in range(1, count - step + 1)])
        whole = add_at(whole, from_left, me - step, last)
        whole = add_at(whole, from_right, me + step, last)
    return whole


def driven_by_line(inv_parts, noise, axis):
    count = lax.axis_size(axis)
    me = lax.axis_index(axis)
    rows = noise.shape[1] // count

    def own_rows(target):
        return lax.dynamic_slice_in_dim(noise, jnp.clip(target, 0, count - 1) * rows, rows, axis=1)

    def partial(piece):
        return jnp.stack([apply(inv_parts[block], piece[block]) for block in range(noise.shape[0])], axis=0)

    from_left = {}
    from_right = {}
    for distance in range(count - 1, 0, -1):
        from_left[distance] = lax.ppermute(
            own_rows(me + distance), axis, [(k, k + distance) for k in range(0, count - distance)]
        )
        from_right[distance] = lax.ppermute(
            own_rows(me - distance), axis, [(k, k - distance) for k in range(distance, count)]
        )
    rightward = None
    leftward = None
    for step in range(1, count):
        right_route = [(k, k + 1) for k in range(0, min(step, count - 1))]
        left_route = [(k, k - 1) for k in range(max(count - step, 1), count)]
        going_right = partial(from_right[count - step])
        going_left = partial(from_left[count - step])
        if rightward is not None:
            going_right = going_right + rightward
            going_left = going_left + leftward
        rightward = lax.ppermute(going_right, axis, right_route)
        leftward = lax.ppermute(going_left, axis, left_route)
    own = partial(own_rows(me))
    if rightward is None:
        return own
    return own + (rightward + leftward)


def shards(noise, inv_diag, coupling, order):
    block_count = noise.shape[0]
    node_count = noise.shape[1]
    sample_count = noise.shape[2]
    coupling_full = line_all_gather(coupling, "cols")
    inv_parts = [split(inv_diag[block], 2) for block in range(block_count)]
    driven_all = driven_by_line(inv_parts, noise, "cols")
    driven = [driven_all[block] for block in range(block_count)]
    coupling_parts = [split(coupling_full[block], 2) for block in range(block_count)]

    def chain(entering, skip_last):
        carried = entering
        results = [None] * block_count
        for block in range(block_count - 1, -1, -1):
            if skip_last and block == block_count - 1:
                carried = driven[block]
            else:
                carried = driven[block] + apply(coupling_parts[block], carried)
            results[block] = carried
        return results

    relays = lax.axis_size("tm")
    entering = jnp.zeros_like(driven[0])
    for step in range(relays - 1):
        sender = relays - 1 - step
        leaving = chain(entering, step == 0)[0]
        entering = entering + lax.ppermute(leaving, "tm", [(sender, sender - 1)])
    finals = chain(entering, False)
    selector = (order[:, None] == jnp.arange(node_count, dtype=order.dtype)[None, :]).astype(low)
    pieces = [part for block in range(block_count) for part in split(finals[block], 3)]
    picked = bdot(selector, jnp.concatenate(pieces, axis=1))
    outputs = []
    for block in range(block_count):
        base = 3 * block * sample_count
        top = picked[:, base:base + sample_count]
        middle = picked[:, base + sample_count:base + 2 * sample_count]
        bottom = picked[:, base + 2 * sample_count:base + 3 * sample_count]
        outputs.append(top + (middle + bottom))
    return jnp.stack(outputs, axis=0)


def solution(mesh):
    return jax.shard_map(
        shards,
        mesh=mesh,
        in_specs=(
            P(("parts", "tm"), None, "cols"),
            P(("parts", "tm"), None, "cols"),
            P(("parts", "tm"), None, "cols"),
            P(),
        ),
        out_specs=P(("parts", "tm"), None, "cols"),
        check_vma=False,
    )
```

```python
import jax
import jax.numpy as jnp
from jax import lax
from jax.sharding import PartitionSpec as P

low = jnp.bfloat16


def shifted(block, axis, distance):
    devices = range(lax.axis_size(axis))
    route = [(i - distance, i) for i in devices if i - distance in devices]
    return lax.ppermute(block, axis, route)


def split(value, count):
    parts = []
    rest = value
    for index in range(count):
        kept = lax.reduce_precision(rest, exponent_bits=8, mantissa_bits=7)
        parts.append(kept.astype(low))
        if index < count - 1:
            rest = rest - kept
    return parts


def bdot(left, right):
    return jnp.dot(left, right, preferred_element_type=jnp.float32)


def apply(matrix_parts, operand):
    high, small = matrix_parts
    width = operand.shape[1]
    operand_high, operand_small = split(operand, 2)
    both = bdot(high, jnp.concatenate([operand_high, operand_small], axis=1))
    return both[:, :width] + (both[:, width:] + bdot(small, operand_high))


def line_reduce_scatter(partial, axis):
    count = lax.axis_size(axis)
    me = lax.axis_index(axis)
    width = partial.shape[2] // count

    def tile(owner):
        owner = jnp.clip(owner, 0, count - 1)
        return lax.dynamic_slice_in_dim(partial, owner * width, width, axis=2)

    rightward = jnp.zeros_like(tile(me))
    leftward = jnp.zeros_like(tile(me))
    for step in range(1, count):
        right_route = [(k, k + 1) for k in range(0, min(step, count - 1))]
        left_route = [(k, k - 1) for k in range(max(count - step, 1), count)]
        rightward = lax.ppermute(tile(me + count - step) + rightward, axis, right_route)
        leftward = lax.ppermute(tile(me - count + step) + leftward, axis, left_route)
    return tile(me) + (rightward + leftward)


def add_at(whole, piece, slot, axis):
    count = whole.shape[axis] // piece.shape[axis]
    start = jnp.clip(slot, 0, count - 1) * piece.shape[axis]
    current = lax.dynamic_slice_in_dim(whole, start, piece.shape[axis], axis=axis)
    return lax.dynamic_update_slice_in_dim(whole, current + piece, start, axis=axis)


def line_all_gather(tile, axis):
    count = lax.axis_size(axis)
    me = lax.axis_index(axis)
    last = tile.ndim - 1
    shape = tile.shape[:-1] + (count * tile.shape[-1],)
    whole = add_at(jnp.zeros(shape, tile.dtype), tile, me, last)
    from_left = tile
    from_right = tile
    for step in range(1, count):
        from_left = lax.ppermute(from_left, axis, [(k, k + 1) for k in range(step - 1, count - 1)])
        from_right = lax.ppermute(from_right, axis, [(k, k - 1) for k in range(1, count - step + 1)])
        whole = add_at(whole, from_left, me - step, last)
        whole = add_at(whole, from_right, me + step, last)
    return whole


def line_all_to_all(value, axis):
    count = lax.axis_size(axis)
    me = lax.axis_index(axis)
    rows = value.shape[1] // count

    def own_rows(target):
        return lax.dynamic_slice_in_dim(value, jnp.clip(target, 0, count - 1) * rows, rows, axis=1)

    shape = (value.shape[0], rows, count * value.shape[2])
    whole = add_at(jnp.zeros(shape, value.dtype), own_rows(me), me, 2)
    for distance in range(1, count):
        right = lax.ppermute(own_rows(me + distance), axis, [(k, k + distance) for k in range(0, count - distance)])
        left = lax.ppermute(own_rows(me - distance), axis, [(k, k - distance) for k in range(distance, count)])
        whole = add_at(whole, right, me - distance, 2)
        whole = add_at(whole, left, me + distance, 2)
    return whole


def shards(noise, inv_diag, coupling, order):
    block_count = noise.shape[0]
    node_count = noise.shape[1]
    sample_count = noise.shape[2]
    coupling_full = line_all_gather(coupling, "cols")
    noise_rows = line_all_to_all(noise, "cols")
    partial = jnp.stack(
        [apply(split(inv_diag[block], 2), noise_rows[block]) for block in range(block_count)], axis=0
    )
    driven_all = line_reduce_scatter(partial, "cols")
    driven = [driven_all[block] for block in range(block_count)]
    coupling_parts = [split(coupling_full[block], 2) for block in range(block_count)]

    def chain(entering, skip_last):
        carried = entering
        results = [None] * block_count
        for block in range(block_count - 1, -1, -1):
            if skip_last and block == block_count - 1:
                carried = driven[block]
            else:
                carried = driven[block] + apply(coupling_parts[block], carried)
            results[block] = carried
        return results

    across = coupling_full[block_count - 1]
    for block in range(block_count - 2, -1, -1):
        across = apply(coupling_parts[block], across)
    across_parts = split(across, 2)
    local = chain(None, True)[0]
    relays = lax.axis_size("tm")
    entering = jnp.zeros_like(driven[0])
    for step in range(relays - 1):
        sender = relays - 1 - step
        leaving = local if step == 0 else local + apply(across_parts, entering)
        entering = entering + lax.ppermute(leaving, "tm", [(sender, sender - 1)])
    finals = chain(entering, False)
    selector = (order[:, None] == jnp.arange(node_count, dtype=order.dtype)[None, :]).astype(low)
    pieces = [part for block in range(block_count) for part in split(finals[block], 3)]
    picked = bdot(selector, jnp.concatenate(pieces, axis=1))
    outputs = []
    for block in range(block_count):
        base = 3 * block * sample_count
        top = picked[:, base:base + sample_count]
        middle = picked[:, base + sample_count:base + 2 * sample_count]
        bottom = picked[:, base + 2 * sample_count:base + 3 * sample_count]
        outputs.append(top + (middle + bottom))
    return jnp.stack(outputs, axis=0)


def solution(mesh):
    return jax.shard_map(
        shards,
        mesh=mesh,
        in_specs=(
            P(("parts", "tm"), None, "cols"),
            P(("parts", "tm"), None, "cols"),
            P(("parts", "tm"), None, "cols"),
            P(),
        ),
        out_specs=P(("parts", "tm"), None, "cols"),
        check_vma=False,
    )
```

```python
import jax
import jax.numpy as jnp
from jax import lax
from jax.sharding import PartitionSpec as P

low = jnp.bfloat16


def shifted(block, axis, distance):
    devices = range(lax.axis_size(axis))
    route = [(i - distance, i) for i in devices if i - distance in devices]
    return lax.ppermute(block, axis, route)


def split(value, count):
    parts = []
    rest = value
    for index in range(count):
        kept = lax.reduce_precision(rest, exponent_bits=8, mantissa_bits=7)
        parts.append(kept.astype(low))
        if index < count - 1:
            rest = rest - kept
    return parts


def bdot(left, right):
    return jnp.dot(left, right, preferred_element_type=jnp.float32)


def apply(matrix_parts, operand):
    high, small = matrix_parts
    width = operand.shape[1]
    operand_high, operand_small = split(operand, 2)
    both = bdot(high, jnp.concatenate([operand_high, operand_small], axis=1))
    return both[:, :width] + (both[:, width:] + bdot(small, operand_high))


def line_reduce_scatter(partial, axis):
    count = lax.axis_size(axis)
    me = lax.axis_index(axis)
    width = partial.shape[2] // count

    def tile(owner):
        owner = jnp.clip(owner, 0, count - 1)
        return lax.dynamic_slice_in_dim(partial, owner * width, width, axis=2)

    rightward = jnp.zeros_like(tile(me))
    leftward = jnp.zeros_like(tile(me))
    for step in range(1, count):
        right_route = [(k, k + 1) for k in range(0, min(step, count - 1))]
        left_route = [(k, k - 1) for k in range(max(count - step, 1), count)]
        rightward = lax.ppermute(tile(me + count - step) + rightward, axis, right_route)
        leftward = lax.ppermute(tile(me - count + step) + leftward, axis, left_route)
    return tile(me) + (rightward + leftward)


def add_at(whole, piece, slot, axis):
    count = whole.shape[axis] // piece.shape[axis]
    start = jnp.clip(slot, 0, count - 1) * piece.shape[axis]
    current = lax.dynamic_slice_in_dim(whole, start, piece.shape[axis], axis=axis)
    return lax.dynamic_update_slice_in_dim(whole, current + piece, start, axis=axis)


def line_all_gather(tile, axis, rider=None):
    count = lax.axis_size(axis)
    me = lax.axis_index(axis)
    last = tile.ndim - 1
    shape = tile.shape[:-1] + (count * tile.shape[-1],)
    whole = add_at(jnp.zeros(shape, tile.dtype), tile, me, last)
    from_left = tile
    from_right = tile
    riders = None
    for step in range(1, count):
        right_route = [(k, k + 1) for k in range(step - 1, count - 1)]
        left_route = [(k, k - 1) for k in range(1, count - step + 1)]
        if step == 1 and rider is not None and rider[0].shape[2] != tile.shape[2]:
            riders = (lax.ppermute(rider[0], axis, right_route), lax.ppermute(rider[1], axis, left_route))
        if step == 1 and rider is not None and rider[0].shape[2] == tile.shape[2]:
            rows = tile.shape[1]
            both_left = lax.ppermute(jnp.concatenate([from_left, rider[0]], axis=1), axis, right_route)
            both_right = lax.ppermute(jnp.concatenate([from_right, rider[1]], axis=1), axis, left_route)
            from_left, from_left_rider = both_left[:, :rows], both_left[:, rows:]
            from_right, from_right_rider = both_right[:, :rows], both_right[:, rows:]
            riders = (from_left_rider, from_right_rider)
        if not (step == 1 and rider is not None and rider[0].shape[2] == tile.shape[2]):
            from_left = lax.ppermute(from_left, axis, right_route)
            from_right = lax.ppermute(from_right, axis, left_route)
        whole = add_at(whole, from_left, me - step, last)
        whole = add_at(whole, from_right, me + step, last)
    return whole, riders


def line_all_to_all(value, axis, near):
    count = lax.axis_size(axis)
    me = lax.axis_index(axis)
    rows = value.shape[1] // count

    def own_rows(target):
        return lax.dynamic_slice_in_dim(value, jnp.clip(target, 0, count - 1) * rows, rows, axis=1)

    shape = (value.shape[0], rows, count * value.shape[2])
    whole = add_at(jnp.zeros(shape, value.dtype), own_rows(me), me, 2)
    for distance in range(1, count):
        if distance == 1:
            right, left = near
        else:
            right = lax.ppermute(own_rows(me + distance), axis, [(k, k + distance) for k in range(0, count - distance)])
            left = lax.ppermute(own_rows(me - distance), axis, [(k, k - distance) for k in range(distance, count)])
        whole = add_at(whole, right, me - distance, 2)
        whole = add_at(whole, left, me + distance, 2)
    return whole


def near_rows(value, axis):
    count = lax.axis_size(axis)
    me = lax.axis_index(axis)
    rows = value.shape[1] // count

    def own_rows(target):
        return lax.dynamic_slice_in_dim(value, jnp.clip(target, 0, count - 1) * rows, rows, axis=1)

    return own_rows(me + 1), own_rows(me - 1)


def shards(noise, inv_diag, coupling, order):
    block_count = noise.shape[0]
    node_count = noise.shape[1]
    sample_count = noise.shape[2]
    coupling_full, near = line_all_gather(coupling, "cols", near_rows(noise, "cols"))
    noise_rows = line_all_to_all(noise, "cols", near)
    partial = jnp.stack(
        [apply(split(inv_diag[block], 2), noise_rows[block]) for block in range(block_count)], axis=0
    )
    driven_all = line_reduce_scatter(partial, "cols")
    driven = [driven_all[block] for block in range(block_count)]
    coupling_parts = [split(coupling_full[block], 2) for block in range(block_count)]

    def chain(entering, skip_last):
        carried = entering
        results = [None] * block_count
        for block in range(block_count - 1, -1, -1):
            if skip_last and block == block_count - 1:
                carried = driven[block]
            else:
                carried = driven[block] + apply(coupling_parts[block], carried)
            results[block] = carried
        return results

    relays = lax.axis_size("tm")
    entering = jnp.zeros_like(driven[0])
    for step in range(relays - 1):
        sender = relays - 1 - step
        leaving = chain(entering, step == 0)[0]
        entering = entering + lax.ppermute(leaving, "tm", [(sender, sender - 1)])
    finals = chain(entering, False)
    selector = (order[:, None] == jnp.arange(node_count, dtype=order.dtype)[None, :]).astype(low)
    pieces = [part for block in range(block_count) for part in split(finals[block], 3)]
    picked = bdot(selector, jnp.concatenate(pieces, axis=1))
    outputs = []
    for block in range(block_count):
        base = 3 * block * sample_count
        top = picked[:, base:base + sample_count]
        middle = picked[:, base + sample_count:base + 2 * sample_count]
        bottom = picked[:, base + 2 * sample_count:base + 3 * sample_count]
        outputs.append(top + (middle + bottom))
    return jnp.stack(outputs, axis=0)


def solution(mesh):
    return jax.shard_map(
        shards,
        mesh=mesh,
        in_specs=(
            P(("parts", "tm"), None, "cols"),
            P(("parts", "tm"), None, "cols"),
            P(("parts", "tm"), None, "cols"),
            P(),
        ),
        out_specs=P(("parts", "tm"), None, "cols"),
        check_vma=False,
    )
```

```python
import jax
import jax.numpy as jnp
from jax import lax
from jax.sharding import PartitionSpec as P

low = jnp.bfloat16


def shifted(block, axis, distance):
    devices = range(lax.axis_size(axis))
    route = [(i - distance, i) for i in devices if i - distance in devices]
    return lax.ppermute(block, axis, route)


def split(value, count):
    parts = []
    rest = value
    for index in range(count):
        kept = lax.reduce_precision(rest, exponent_bits=8, mantissa_bits=7)
        parts.append(kept.astype(low))
        if index < count - 1:
            rest = rest - kept
    return parts


def bdot(left, right):
    return jnp.dot(left, right, preferred_element_type=jnp.float32)


def apply(matrix_parts, operand):
    high, small = matrix_parts
    width = operand.shape[1]
    operand_high, operand_small = split(operand, 2)
    both = bdot(high, jnp.concatenate([operand_high, operand_small], axis=1))
    return both[:, :width] + (both[:, width:] + bdot(small, operand_high))


def line_reduce_scatter(partial, axis):
    count = lax.axis_size(axis)
    me = lax.axis_index(axis)
    width = partial.shape[2] // count

    def tile(owner):
        owner = jnp.clip(owner, 0, count - 1)
        return lax.dynamic_slice_in_dim(partial, owner * width, width, axis=2)

    rightward = jnp.zeros_like(tile(me))
    leftward = jnp.zeros_like(tile(me))
    for step in range(1, count):
        right_route = [(k, k + 1) for k in range(0, min(step, count - 1))]
        left_route = [(k, k - 1) for k in range(max(count - step, 1), count)]
        rightward = lax.ppermute(tile(me + count - step) + rightward, axis, right_route)
        leftward = lax.ppermute(tile(me - count + step) + leftward, axis, left_route)
    return tile(me) + (rightward + leftward)


def add_at(whole, piece, slot, axis):
    count = whole.shape[axis] // piece.shape[axis]
    start = jnp.clip(slot, 0, count - 1) * piece.shape[axis]
    current = lax.dynamic_slice_in_dim(whole, start, piece.shape[axis], axis=axis)
    return lax.dynamic_update_slice_in_dim(whole, current + piece, start, axis=axis)


def line_all_gather(tile, axis):
    count = lax.axis_size(axis)
    me = lax.axis_index(axis)
    last = tile.ndim - 1
    shape = tile.shape[:-1] + (count * tile.shape[-1],)
    whole = add_at(jnp.zeros(shape, tile.dtype), tile, me, last)
    from_left = tile
    from_right = tile
    for step in range(1, count):
        from_left = lax.ppermute(from_left, axis, [(k, k + 1) for k in range(step - 1, count - 1)])
        from_right = lax.ppermute(from_right, axis, [(k, k - 1) for k in range(1, count - step + 1)])
        whole = add_at(whole, from_left, me - step, last)
        whole = add_at(whole, from_right, me + step, last)
    return whole


def line_all_to_all(value, axis):
    count = lax.axis_size(axis)
    me = lax.axis_index(axis)
    rows = value.shape[1] // count

    def own_rows(target):
        return lax.dynamic_slice_in_dim(value, jnp.clip(target, 0, count - 1) * rows, rows, axis=1)

    shape = (value.shape[0], rows, count * value.shape[2])
    whole = add_at(jnp.zeros(shape, value.dtype), own_rows(me), me, 2)
    for distance in range(1, count):
        right = lax.ppermute(own_rows(me + distance), axis, [(k, k + distance) for k in range(0, count - distance)])
        left = lax.ppermute(own_rows(me - distance), axis, [(k, k - distance) for k in range(distance, count)])
        whole = add_at(whole, right, me - distance, 2)
        whole = add_at(whole, left, me + distance, 2)
    return whole


def shards(noise, inv_diag, coupling, order):
    block_count = noise.shape[0]
    node_count = noise.shape[1]
    sample_count = noise.shape[2]
    coupling_full = line_all_gather(coupling, "cols")
    noise_rows = line_all_to_all(noise, "cols")
    partial = jnp.stack(
        [apply(split(inv_diag[block], 2), noise_rows[block]) for block in range(block_count)], axis=0
    )
    driven_all = line_reduce_scatter(partial, "cols")
    driven = [driven_all[block] for block in range(block_count)]
    coupling_parts = [split(coupling_full[block], 2) for block in range(block_count)]

    def chain_columns(entering, skip_last, columns):
        carried = entering
        results = [None] * block_count
        for block in range(block_count - 1, -1, -1):
            if skip_last and block == block_count - 1:
                carried = driven[block][:, columns]
            else:
                carried = driven[block][:, columns] + apply(coupling_parts[block], carried)
            results[block] = carried
        return results

    def chain(entering, skip_last):
        carried = entering
        results = [None] * block_count
        for block in range(block_count - 1, -1, -1):
            if skip_last and block == block_count - 1:
                carried = driven[block]
            else:
                carried = driven[block] + apply(coupling_parts[block], carried)
            results[block] = carried
        return results

    relays = lax.axis_size("tm")
    halves = 2 if sample_count % 256 == 0 else 1
    width = sample_count // halves
    entering = [jnp.zeros_like(driven[0][:, :width]) for _ in range(halves)]
    for step in range(relays - 1):
        sender = relays - 1 - step
        for half in range(halves):
            columns = slice(half * width, (half + 1) * width)
            leaving = chain_columns(entering[half], step == 0, columns)[0]
            entering[half] = entering[half] + lax.ppermute(leaving, "tm", [(sender, sender - 1)])
    finals = chain(jnp.concatenate(entering, axis=1), False)
    selector = (order[:, None] == jnp.arange(node_count, dtype=order.dtype)[None, :]).astype(low)
    pieces = [part for block in range(block_count) for part in split(finals[block], 3)]
    picked = bdot(selector, jnp.concatenate(pieces, axis=1))
    outputs = []
    for block in range(block_count):
        base = 3 * block * sample_count
        top = picked[:, base:base + sample_count]
        middle = picked[:, base + sample_count:base + 2 * sample_count]
        bottom = picked[:, base + 2 * sample_count:base + 3 * sample_count]
        outputs.append(top + (middle + bottom))
    return jnp.stack(outputs, axis=0)


def solution(mesh):
    return jax.shard_map(
        shards,
        mesh=mesh,
        in_specs=(
            P(("parts", "tm"), None, "cols"),
            P(("parts", "tm"), None, "cols"),
            P(("parts", "tm"), None, "cols"),
            P(),
        ),
        out_specs=P(("parts", "tm"), None, "cols"),
        check_vma=False,
    )
```

```python
import jax
import jax.numpy as jnp
from jax import lax
from jax.sharding import PartitionSpec as P
from jax.experimental import pallas as pl
from jax.experimental.pallas import tpu as pltpu

low = jnp.bfloat16


def shifted(block, axis, distance):
    devices = range(lax.axis_size(axis))
    route = [(i - distance, i) for i in devices if i - distance in devices]
    return lax.ppermute(block, axis, route)


def split(value, count):
    parts = []
    rest = value
    for index in range(count):
        kept = lax.reduce_precision(rest, exponent_bits=8, mantissa_bits=7)
        parts.append(kept.astype(low))
        if index < count - 1:
            rest = rest - kept
    return parts


def bdot(left, right):
    return jnp.dot(left, right, preferred_element_type=jnp.float32)


def apply(matrix_parts, operand):
    high, small = matrix_parts
    width = operand.shape[1]
    operand_high, operand_small = split(operand, 2)
    both = bdot(high, jnp.concatenate([operand_high, operand_small], axis=1))
    return both[:, :width] + (both[:, width:] + bdot(small, operand_high))


def line_reduce_scatter(partial, axis):
    count = lax.axis_size(axis)
    me = lax.axis_index(axis)
    width = partial.shape[2] // count

    def tile(owner):
        owner = jnp.clip(owner, 0, count - 1)
        return lax.dynamic_slice_in_dim(partial, owner * width, width, axis=2)

    rightward = jnp.zeros_like(tile(me))
    leftward = jnp.zeros_like(tile(me))
    for step in range(1, count):
        right_route = [(k, k + 1) for k in range(0, min(step, count - 1))]
        left_route = [(k, k - 1) for k in range(max(count - step, 1), count)]
        rightward = lax.ppermute(tile(me + count - step) + rightward, axis, right_route)
        leftward = lax.ppermute(tile(me - count + step) + leftward, axis, left_route)
    return tile(me) + (rightward + leftward)


def add_at(whole, piece, slot, axis):
    count = whole.shape[axis] // piece.shape[axis]
    start = jnp.clip(slot, 0, count - 1) * piece.shape[axis]
    current = lax.dynamic_slice_in_dim(whole, start, piece.shape[axis], axis=axis)
    return lax.dynamic_update_slice_in_dim(whole, current + piece, start, axis=axis)


def line_all_gather(tile, axis):
    count = lax.axis_size(axis)
    me = lax.axis_index(axis)
    last = tile.ndim - 1
    shape = tile.shape[:-1] + (count * tile.shape[-1],)
    whole = add_at(jnp.zeros(shape, tile.dtype), tile, me, last)
    from_left = tile
    from_right = tile
    for step in range(1, count):
        from_left = lax.ppermute(from_left, axis, [(k, k + 1) for k in range(step - 1, count - 1)])
        from_right = lax.ppermute(from_right, axis, [(k, k - 1) for k in range(1, count - step + 1)])
        whole = add_at(whole, from_left, me - step, last)
        whole = add_at(whole, from_right, me + step, last)
    return whole


def line_all_to_all(value, axis):
    count = lax.axis_size(axis)
    me = lax.axis_index(axis)
    rows = value.shape[1] // count

    def own_rows(target):
        return lax.dynamic_slice_in_dim(value, jnp.clip(target, 0, count - 1) * rows, rows, axis=1)

    shape = (value.shape[0], rows, count * value.shape[2])
    whole = add_at(jnp.zeros(shape, value.dtype), own_rows(me), me, 2)
    for distance in range(1, count):
        right = lax.ppermute(own_rows(me + distance), axis, [(k, k + distance) for k in range(0, count - distance)])
        left = lax.ppermute(own_rows(me - distance), axis, [(k, k - distance) for k in range(distance, count)])
        whole = add_at(whole, right, me - distance, 2)
        whole = add_at(whole, left, me + distance, 2)
    return whole


def pick_rows_kernel(order_ref, field_ref, out_ref):
    blocks = field_ref.shape[0]

    def body(row, carry):
        source = order_ref[row]
        for block in range(blocks):
            out_ref[block, pl.ds(row, 1), :] = field_ref[block, pl.ds(source, 1), :]
        return carry

    lax.fori_loop(0, field_ref.shape[1], body, 0, unroll=8)


def pick_rows(field, order):
    return pl.pallas_call(
        pick_rows_kernel,
        out_shape=jax.ShapeDtypeStruct(field.shape, field.dtype),
        in_specs=[pl.BlockSpec(memory_space=pltpu.SMEM), pl.BlockSpec(memory_space=pltpu.VMEM)],
        out_specs=pl.BlockSpec(memory_space=pltpu.VMEM),
        cost_estimate=pl.CostEstimate(flops=0, transcendentals=0, bytes_accessed=2 * field.size * 4),
    )(order, field)


def shards(noise, inv_diag, coupling, order):
    block_count = noise.shape[0]
    node_count = noise.shape[1]
    sample_count = noise.shape[2]
    coupling_full = line_all_gather(coupling, "cols")
    noise_rows = line_all_to_all(noise, "cols")
    partial = jnp.stack(
        [apply(split(inv_diag[block], 2), noise_rows[block]) for block in range(block_count)], axis=0
    )
    driven_all = line_reduce_scatter(partial, "cols")
    driven = [driven_all[block] for block in range(block_count)]
    coupling_parts = [split(coupling_full[block], 2) for block in range(block_count)]

    def chain(entering, skip_last):
        carried = entering
        results = [None] * block_count
        for block in range(block_count - 1, -1, -1):
            if skip_last and block == block_count - 1:
                carried = driven[block]
            else:
                carried = driven[block] + apply(coupling_parts[block], carried)
            results[block] = carried
        return results

    relays = lax.axis_size("tm")
    entering = jnp.zeros_like(driven[0])
    for step in range(relays - 1):
        sender = relays - 1 - step
        leaving = chain(entering, step == 0)[0]
        entering = entering + lax.ppermute(leaving, "tm", [(sender, sender - 1)])
    finals = chain(entering, False)
    return pick_rows(jnp.stack(finals, axis=0), order)


def solution(mesh):
    return jax.shard_map(
        shards,
        mesh=mesh,
        in_specs=(
            P(("parts", "tm"), None, "cols"),
            P(("parts", "tm"), None, "cols"),
            P(("parts", "tm"), None, "cols"),
            P(),
        ),
        out_specs=P(("parts", "tm"), None, "cols"),
        check_vma=False,
    )
```

```python
import jax
import jax.numpy as jnp
from jax import lax
from jax.sharding import PartitionSpec as P
from jax.experimental import pallas as pl
from jax.experimental.pallas import tpu as pltpu

low = jnp.bfloat16


def shifted(block, axis, distance):
    devices = range(lax.axis_size(axis))
    route = [(i - distance, i) for i in devices if i - distance in devices]
    return lax.ppermute(block, axis, route)


def split(value, count):
    parts = []
    rest = value
    for index in range(count):
        kept = lax.reduce_precision(rest, exponent_bits=8, mantissa_bits=7)
        parts.append(kept.astype(low))
        if index < count - 1:
            rest = rest - kept
    return parts


def bdot(left, right):
    return jnp.dot(left, right, preferred_element_type=jnp.float32)


def apply(matrix_parts, operand):
    high, small = matrix_parts
    width = operand.shape[1]
    operand_high, operand_small = split(operand, 2)
    both = bdot(high, jnp.concatenate([operand_high, operand_small], axis=1))
    return both[:, :width] + (both[:, width:] + bdot(small, operand_high))


def line_reduce_scatter(partial, axis):
    count = lax.axis_size(axis)
    me = lax.axis_index(axis)
    width = partial.shape[2] // count

    def tile(owner):
        owner = jnp.clip(owner, 0, count - 1)
        return lax.dynamic_slice_in_dim(partial, owner * width, width, axis=2)

    rightward = jnp.zeros_like(tile(me))
    leftward = jnp.zeros_like(tile(me))
    for step in range(1, count):
        right_route = [(k, k + 1) for k in range(0, min(step, count - 1))]
        left_route = [(k, k - 1) for k in range(max(count - step, 1), count)]
        rightward = lax.ppermute(tile(me + count - step) + rightward, axis, right_route)
        leftward = lax.ppermute(tile(me - count + step) + leftward, axis, left_route)
    return tile(me) + (rightward + leftward)


def add_at(whole, piece, slot, axis):
    count = whole.shape[axis] // piece.shape[axis]
    start = jnp.clip(slot, 0, count - 1) * piece.shape[axis]
    current = lax.dynamic_slice_in_dim(whole, start, piece.shape[axis], axis=axis)
    return lax.dynamic_update_slice_in_dim(whole, current + piece, start, axis=axis)


def line_all_gather(tile, axis):
    count = lax.axis_size(axis)
    me = lax.axis_index(axis)
    last = tile.ndim - 1
    shape = tile.shape[:-1] + (count * tile.shape[-1],)
    whole = add_at(jnp.zeros(shape, tile.dtype), tile, me, last)
    from_left = tile
    from_right = tile
    for step in range(1, count):
        from_left = lax.ppermute(from_left, axis, [(k, k + 1) for k in range(step - 1, count - 1)])
        from_right = lax.ppermute(from_right, axis, [(k, k - 1) for k in range(1, count - step + 1)])
        whole = add_at(whole, from_left, me - step, last)
        whole = add_at(whole, from_right, me + step, last)
    return whole


def line_all_to_all(value, axis):
    count = lax.axis_size(axis)
    me = lax.axis_index(axis)
    rows = value.shape[1] // count

    def own_rows(target):
        return lax.dynamic_slice_in_dim(value, jnp.clip(target, 0, count - 1) * rows, rows, axis=1)

    shape = (value.shape[0], rows, count * value.shape[2])
    whole = add_at(jnp.zeros(shape, value.dtype), own_rows(me), me, 2)
    for distance in range(1, count):
        right = lax.ppermute(own_rows(me + distance), axis, [(k, k + distance) for k in range(0, count - distance)])
        left = lax.ppermute(own_rows(me - distance), axis, [(k, k - distance) for k in range(distance, count)])
        whole = add_at(whole, right, me - distance, 2)
        whole = add_at(whole, left, me + distance, 2)
    return whole


def pick_rows_kernel(order_ref, field_ref, out_ref):
    blocks = field_ref.shape[0]
    group = 8

    def body(index, carry):
        start = pl.multiple_of(index * group, group)
        sources = [order_ref[start + row] for row in range(group)]
        for block in range(blocks):
            rows = [field_ref[block, pl.ds(source, 1), :] for source in sources]
            out_ref[block, pl.ds(start, group), :] = jnp.concatenate(rows, axis=0)
        return carry

    lax.fori_loop(0, field_ref.shape[1] // group, body, 0, unroll=2)


def pick_rows(field, order):
    return pl.pallas_call(
        pick_rows_kernel,
        out_shape=jax.ShapeDtypeStruct(field.shape, field.dtype),
        in_specs=[pl.BlockSpec(memory_space=pltpu.SMEM), pl.BlockSpec(memory_space=pltpu.VMEM)],
        out_specs=pl.BlockSpec(memory_space=pltpu.VMEM),
        cost_estimate=pl.CostEstimate(flops=0, transcendentals=0, bytes_accessed=2 * field.size * 4),
    )(order, field)


def shards(noise, inv_diag, coupling, order):
    block_count = noise.shape[0]
    node_count = noise.shape[1]
    sample_count = noise.shape[2]
    coupling_full = line_all_gather(coupling, "cols")
    noise_rows = line_all_to_all(noise, "cols")
    partial = jnp.stack(
        [apply(split(inv_diag[block], 2), noise_rows[block]) for block in range(block_count)], axis=0
    )
    driven_all = line_reduce_scatter(partial, "cols")
    driven = [driven_all[block] for block in range(block_count)]
    coupling_parts = [split(coupling_full[block], 2) for block in range(block_count)]

    def chain(entering, skip_last):
        carried = entering
        results = [None] * block_count
        for block in range(block_count - 1, -1, -1):
            if skip_last and block == block_count - 1:
                carried = driven[block]
            else:
                carried = driven[block] + apply(coupling_parts[block], carried)
            results[block] = carried
        return results

    relays = lax.axis_size("tm")
    entering = jnp.zeros_like(driven[0])
    for step in range(relays - 1):
        sender = relays - 1 - step
        leaving = chain(entering, step == 0)[0]
        entering = entering + lax.ppermute(leaving, "tm", [(sender, sender - 1)])
    finals = chain(entering, False)
    return pick_rows(jnp.stack(finals, axis=0), order)


def solution(mesh):
    return jax.shard_map(
        shards,
        mesh=mesh,
        in_specs=(
            P(("parts", "tm"), None, "cols"),
            P(("parts", "tm"), None, "cols"),
            P(("parts", "tm"), None, "cols"),
            P(),
        ),
        out_specs=P(("parts", "tm"), None, "cols"),
        check_vma=False,
    )
```

```python
import jax
import jax.numpy as jnp
from jax import lax
from jax.sharding import PartitionSpec as P
from jax.experimental import pallas as pl
from jax.experimental.pallas import tpu as pltpu

low = jnp.bfloat16


def shifted(block, axis, distance):
    devices = range(lax.axis_size(axis))
    route = [(i - distance, i) for i in devices if i - distance in devices]
    return lax.ppermute(block, axis, route)


def split(value, count):
    parts = []
    rest = value
    for index in range(count):
        kept = lax.reduce_precision(rest, exponent_bits=8, mantissa_bits=7)
        parts.append(kept.astype(low))
        if index < count - 1:
            rest = rest - kept
    return parts


def bdot(left, right):
    return jnp.dot(left, right, preferred_element_type=jnp.float32)


def apply(matrix_parts, operand):
    high, small = matrix_parts
    width = operand.shape[1]
    operand_high, operand_small = split(operand, 2)
    both = bdot(high, jnp.concatenate([operand_high, operand_small], axis=1))
    return both[:, :width] + (both[:, width:] + bdot(small, operand_high))


def line_reduce_scatter(partial, axis):
    count = lax.axis_size(axis)
    me = lax.axis_index(axis)
    width = partial.shape[2] // count

    def tile(owner):
        owner = jnp.clip(owner, 0, count - 1)
        return lax.dynamic_slice_in_dim(partial, owner * width, width, axis=2)

    rightward = jnp.zeros_like(tile(me))
    leftward = jnp.zeros_like(tile(me))
    for step in range(1, count):
        right_route = [(k, k + 1) for k in range(0, min(step, count - 1))]
        left_route = [(k, k - 1) for k in range(max(count - step, 1), count)]
        rightward = lax.ppermute(tile(me + count - step) + rightward, axis, right_route)
        leftward = lax.ppermute(tile(me - count + step) + leftward, axis, left_route)
    return tile(me) + (rightward + leftward)


def add_at(whole, piece, slot, axis):
    count = whole.shape[axis] // piece.shape[axis]
    start = jnp.clip(slot, 0, count - 1) * piece.shape[axis]
    current = lax.dynamic_slice_in_dim(whole, start, piece.shape[axis], axis=axis)
    return lax.dynamic_update_slice_in_dim(whole, current + piece, start, axis=axis)


def line_all_gather(tile, axis):
    count = lax.axis_size(axis)
    me = lax.axis_index(axis)
    last = tile.ndim - 1
    shape = tile.shape[:-1] + (count * tile.shape[-1],)
    whole = add_at(jnp.zeros(shape, tile.dtype), tile, me, last)
    from_left = tile
    from_right = tile
    for step in range(1, count):
        from_left = lax.ppermute(from_left, axis, [(k, k + 1) for k in range(step - 1, count - 1)])
        from_right = lax.ppermute(from_right, axis, [(k, k - 1) for k in range(1, count - step + 1)])
        whole = add_at(whole, from_left, me - step, last)
        whole = add_at(whole, from_right, me + step, last)
    return whole


def line_all_to_all(value, axis):
    count = lax.axis_size(axis)
    me = lax.axis_index(axis)
    rows = value.shape[1] // count

    def own_rows(target):
        return lax.dynamic_slice_in_dim(value, jnp.clip(target, 0, count - 1) * rows, rows, axis=1)

    shape = (value.shape[0], rows, count * value.shape[2])
    whole = add_at(jnp.zeros(shape, value.dtype), own_rows(me), me, 2)
    for distance in range(1, count):
        right = lax.ppermute(own_rows(me + distance), axis, [(k, k + distance) for k in range(0, count - distance)])
        left = lax.ppermute(own_rows(me - distance), axis, [(k, k - distance) for k in range(distance, count)])
        whole = add_at(whole, right, me - distance, 2)
        whole = add_at(whole, left, me + distance, 2)
    return whole


def pick_rows_kernel(order_ref, *refs):
    field_refs = refs[:-1]
    out_ref = refs[-1]
    group = 8

    def body(index, carry):
        start = pl.multiple_of(index * group, group)
        sources = [order_ref[start + row] for row in range(group)]
        for block, field_ref in enumerate(field_refs):
            rows = [field_ref[pl.ds(source, 1), :] for source in sources]
            out_ref[block, pl.ds(start, group), :] = jnp.concatenate(rows, axis=0)
        return carry

    lax.fori_loop(0, out_ref.shape[1] // group, body, 0, unroll=4)


def pick_rows(fields, order):
    shape = (len(fields),) + fields[0].shape
    return pl.pallas_call(
        pick_rows_kernel,
        out_shape=jax.ShapeDtypeStruct(shape, fields[0].dtype),
        in_specs=[pl.BlockSpec(memory_space=pltpu.SMEM)] + [pl.BlockSpec(memory_space=pltpu.VMEM)] * len(fields),
        out_specs=pl.BlockSpec(memory_space=pltpu.VMEM),
        cost_estimate=pl.CostEstimate(flops=0, transcendentals=0, bytes_accessed=2 * len(fields) * fields[0].size * 4),
    )(order, *fields)


def shards(noise, inv_diag, coupling, order):
    block_count = noise.shape[0]
    node_count = noise.shape[1]
    sample_count = noise.shape[2]
    coupling_full = line_all_gather(coupling, "cols")
    noise_rows = line_all_to_all(noise, "cols")
    partial = jnp.stack(
        [apply(split(inv_diag[block], 2), noise_rows[block]) for block in range(block_count)], axis=0
    )
    driven_all = line_reduce_scatter(partial, "cols")
    driven = [driven_all[block] for block in range(block_count)]
    coupling_parts = [split(coupling_full[block], 2) for block in range(block_count)]

    def chain(entering, skip_last):
        carried = entering
        results = [None] * block_count
        for block in range(block_count - 1, -1, -1):
            if skip_last and block == block_count - 1:
                carried = driven[block]
            else:
                carried = driven[block] + apply(coupling_parts[block], carried)
            results[block] = carried
        return results

    relays = lax.axis_size("tm")
    entering = jnp.zeros_like(driven[0])
    for step in range(relays - 1):
        sender = relays - 1 - step
        leaving = chain(entering, step == 0)[0]
        entering = entering + lax.ppermute(leaving, "tm", [(sender, sender - 1)])
    finals = chain(entering, False)
    return pick_rows(finals, order)


def solution(mesh):
    return jax.shard_map(
        shards,
        mesh=mesh,
        in_specs=(
            P(("parts", "tm"), None, "cols"),
            P(("parts", "tm"), None, "cols"),
            P(("parts", "tm"), None, "cols"),
            P(),
        ),
        out_specs=P(("parts", "tm"), None, "cols"),
        check_vma=False,
    )
```

```python
import jax
import jax.numpy as jnp
from jax import lax
from jax.sharding import PartitionSpec as P
from jax.experimental import pallas as pl
from jax.experimental.pallas import tpu as pltpu

low = jnp.bfloat16


def shifted(block, axis, distance):
    devices = range(lax.axis_size(axis))
    route = [(i - distance, i) for i in devices if i - distance in devices]
    return lax.ppermute(block, axis, route)


def split(value, count):
    parts = []
    rest = value
    for index in range(count):
        kept = lax.reduce_precision(rest, exponent_bits=8, mantissa_bits=7)
        parts.append(kept.astype(low))
        if index < count - 1:
            rest = rest - kept
    return parts


def bdot(left, right):
    return jnp.dot(left, right, preferred_element_type=jnp.float32)


def apply(matrix_parts, operand):
    high, small = matrix_parts
    width = operand.shape[1]
    operand_high, operand_small = split(operand, 2)
    both = bdot(high, jnp.concatenate([operand_high, operand_small], axis=1))
    return both[:, :width] + (both[:, width:] + bdot(small, operand_high))


def line_reduce_scatter(partial, axis, ready=None):
    count = lax.axis_size(axis)
    me = lax.axis_index(axis)
    width = partial.shape[2] // count

    def tile(owner):
        owner = jnp.clip(owner, 0, count - 1)
        return lax.dynamic_slice_in_dim(partial, owner * width, width, axis=2)

    rightward = jnp.zeros_like(tile(me))
    leftward = jnp.zeros_like(tile(me))
    for step in range(1, count):
        right_route = [(k, k + 1) for k in range(0, min(step, count - 1))]
        left_route = [(k, k - 1) for k in range(max(count - step, 1), count)]
        rightward = lax.ppermute(tile(me + count - step) + rightward, axis, right_route)
        leftward = lax.ppermute(tile(me - count + step) + leftward, axis, left_route)
    if ready is not None:
        rightward, leftward, ready = lax.optimization_barrier((rightward, leftward, ready))
    return tile(me) + (rightward + leftward), ready


def add_at(whole, piece, slot, axis):
    count = whole.shape[axis] // piece.shape[axis]
    start = jnp.clip(slot, 0, count - 1) * piece.shape[axis]
    current = lax.dynamic_slice_in_dim(whole, start, piece.shape[axis], axis=axis)
    return lax.dynamic_update_slice_in_dim(whole, current + piece, start, axis=axis)


def line_all_gather(tile, axis):
    count = lax.axis_size(axis)
    me = lax.axis_index(axis)
    last = tile.ndim - 1
    shape = tile.shape[:-1] + (count * tile.shape[-1],)
    whole = add_at(jnp.zeros(shape, tile.dtype), tile, me, last)
    from_left = tile
    from_right = tile
    for step in range(1, count):
        from_left = lax.ppermute(from_left, axis, [(k, k + 1) for k in range(step - 1, count - 1)])
        from_right = lax.ppermute(from_right, axis, [(k, k - 1) for k in range(1, count - step + 1)])
        whole = add_at(whole, from_left, me - step, last)
        whole = add_at(whole, from_right, me + step, last)
    return whole


def line_all_to_all(value, axis):
    count = lax.axis_size(axis)
    me = lax.axis_index(axis)
    rows = value.shape[1] // count

    def own_rows(target):
        return lax.dynamic_slice_in_dim(value, jnp.clip(target, 0, count - 1) * rows, rows, axis=1)

    shape = (value.shape[0], rows, count * value.shape[2])
    whole = add_at(jnp.zeros(shape, value.dtype), own_rows(me), me, 2)
    for distance in range(1, count):
        right = lax.ppermute(own_rows(me + distance), axis, [(k, k + distance) for k in range(0, count - distance)])
        left = lax.ppermute(own_rows(me - distance), axis, [(k, k - distance) for k in range(distance, count)])
        whole = add_at(whole, right, me - distance, 2)
        whole = add_at(whole, left, me + distance, 2)
    return whole


def pick_rows_kernel(order_ref, field_ref, out_ref):
    blocks = field_ref.shape[0]
    group = 8

    def body(index, carry):
        start = pl.multiple_of(index * group, group)
        sources = [order_ref[start + row] for row in range(group)]
        for block in range(blocks):
            rows = [field_ref[block, pl.ds(source, 1), :] for source in sources]
            out_ref[block, pl.ds(start, group), :] = jnp.concatenate(rows, axis=0)
        return carry

    lax.fori_loop(0, field_ref.shape[1] // group, body, 0, unroll=2)


def pick_rows(field, order):
    return pl.pallas_call(
        pick_rows_kernel,
        out_shape=jax.ShapeDtypeStruct(field.shape, field.dtype),
        in_specs=[pl.BlockSpec(memory_space=pltpu.SMEM), pl.BlockSpec(memory_space=pltpu.VMEM)],
        out_specs=pl.BlockSpec(memory_space=pltpu.VMEM),
        cost_estimate=pl.CostEstimate(flops=0, transcendentals=0, bytes_accessed=2 * field.size * 4),
    )(order, field)


def shards(noise, inv_diag, coupling, order):
    block_count = noise.shape[0]
    node_count = noise.shape[1]
    sample_count = noise.shape[2]
    coupling_full = line_all_gather(coupling, "cols")
    noise_rows = line_all_to_all(noise, "cols")
    partial = jnp.stack(
        [apply(split(inv_diag[block], 2), noise_rows[block]) for block in range(block_count)], axis=0
    )
    coupling_parts = [split(coupling_full[block], 2) for block in range(block_count)]
    across = coupling_full[block_count - 1]
    for block in range(block_count - 2, -1, -1):
        across = apply(coupling_parts[block], across)
    driven_all, across_parts = line_reduce_scatter(partial, "cols", split(across, 2))
    driven = [driven_all[block] for block in range(block_count)]

    def chain(entering, skip_last):
        carried = entering
        results = [None] * block_count
        for block in range(block_count - 1, -1, -1):
            if skip_last and block == block_count - 1:
                carried = driven[block]
            else:
                carried = driven[block] + apply(coupling_parts[block], carried)
            results[block] = carried
        return results

    local = chain(None, True)[0]
    relays = lax.axis_size("tm")
    entering = jnp.zeros_like(driven[0])
    for step in range(relays - 1):
        sender = relays - 1 - step
        leaving = local if step == 0 else local + apply(across_parts, entering)
        entering = entering + lax.ppermute(leaving, "tm", [(sender, sender - 1)])
    finals = chain(entering, False)
    return pick_rows(jnp.stack(finals, axis=0), order)


def solution(mesh):
    return jax.shard_map(
        shards,
        mesh=mesh,
        in_specs=(
            P(("parts", "tm"), None, "cols"),
            P(("parts", "tm"), None, "cols"),
            P(("parts", "tm"), None, "cols"),
            P(),
        ),
        out_specs=P(("parts", "tm"), None, "cols"),
        check_vma=False,
    )
```

```python
import jax
import jax.numpy as jnp
from jax import lax
from jax.sharding import PartitionSpec as P
from jax.experimental import pallas as pl
from jax.experimental.pallas import tpu as pltpu

low = jnp.bfloat16


def shifted(block, axis, distance):
    devices = range(lax.axis_size(axis))
    route = [(i - distance, i) for i in devices if i - distance in devices]
    return lax.ppermute(block, axis, route)


def split(value, count):
    parts = []
    rest = value
    for index in range(count):
        kept = lax.reduce_precision(rest, exponent_bits=8, mantissa_bits=7)
        parts.append(kept.astype(low))
        if index < count - 1:
            rest = rest - kept
    return parts


def bdot(left, right):
    return jnp.dot(left, right, preferred_element_type=jnp.float32)


def apply(matrix_parts, operand):
    high, small = matrix_parts
    width = operand.shape[1]
    operand_high, operand_small = split(operand, 2)
    both = bdot(high, jnp.concatenate([operand_high, operand_small], axis=1))
    return both[:, :width] + (both[:, width:] + bdot(small, operand_high))


def line_reduce_scatter(partial, axis, ready=None):
    count = lax.axis_size(axis)
    me = lax.axis_index(axis)
    width = partial.shape[2] // count

    def tile(owner):
        owner = jnp.clip(owner, 0, count - 1)
        return lax.dynamic_slice_in_dim(partial, owner * width, width, axis=2)

    rightward = jnp.zeros_like(tile(me))
    leftward = jnp.zeros_like(tile(me))
    for step in range(1, count):
        right_route = [(k, k + 1) for k in range(0, min(step, count - 1))]
        left_route = [(k, k - 1) for k in range(max(count - step, 1), count)]
        rightward = lax.ppermute(tile(me + count - step) + rightward, axis, right_route)
        leftward = lax.ppermute(tile(me - count + step) + leftward, axis, left_route)
    if ready is not None:
        rightward, leftward, ready = lax.optimization_barrier((rightward, leftward, ready))
    return tile(me) + (rightward + leftward), ready


def add_at(whole, piece, slot, axis):
    count = whole.shape[axis] // piece.shape[axis]
    start = jnp.clip(slot, 0, count - 1) * piece.shape[axis]
    current = lax.dynamic_slice_in_dim(whole, start, piece.shape[axis], axis=axis)
    return lax.dynamic_update_slice_in_dim(whole, current + piece, start, axis=axis)


def line_all_gather(tile, axis):
    count = lax.axis_size(axis)
    me = lax.axis_index(axis)
    last = tile.ndim - 1
    shape = tile.shape[:-1] + (count * tile.shape[-1],)
    whole = add_at(jnp.zeros(shape, tile.dtype), tile, me, last)
    from_left = tile
    from_right = tile
    for step in range(1, count):
        from_left = lax.ppermute(from_left, axis, [(k, k + 1) for k in range(step - 1, count - 1)])
        from_right = lax.ppermute(from_right, axis, [(k, k - 1) for k in range(1, count - step + 1)])
        whole = add_at(whole, from_left, me - step, last)
        whole = add_at(whole, from_right, me + step, last)
    return whole


def line_all_to_all(value, axis):
    count = lax.axis_size(axis)
    me = lax.axis_index(axis)
    rows = value.shape[1] // count

    def own_rows(target):
        return lax.dynamic_slice_in_dim(value, jnp.clip(target, 0, count - 1) * rows, rows, axis=1)

    shape = (value.shape[0], rows, count * value.shape[2])
    whole = add_at(jnp.zeros(shape, value.dtype), own_rows(me), me, 2)
    for distance in range(1, count):
        right = lax.ppermute(own_rows(me + distance), axis, [(k, k + distance) for k in range(0, count - distance)])
        left = lax.ppermute(own_rows(me - distance), axis, [(k, k - distance) for k in range(distance, count)])
        whole = add_at(whole, right, me - distance, 2)
        whole = add_at(whole, left, me + distance, 2)
    return whole


def pick_rows_kernel(order_ref, field_ref, out_ref):
    blocks = out_ref.shape[0]
    width = out_ref.shape[2]
    group = 8

    def body(index, carry):
        start = pl.multiple_of(index * group, group)
        rows = jnp.concatenate(
            [field_ref[pl.ds(order_ref[start + row], 1), :] for row in range(group)], axis=0
        )
        for block in range(blocks):
            out_ref[block, pl.ds(start, group), :] = rows[:, block * width:(block + 1) * width]
        return carry

    lax.fori_loop(0, out_ref.shape[1] // group, body, 0, unroll=2)


def pick_rows(fields, order):
    side_by_side = jnp.concatenate(fields, axis=1)
    shape = (len(fields),) + fields[0].shape
    return pl.pallas_call(
        pick_rows_kernel,
        out_shape=jax.ShapeDtypeStruct(shape, fields[0].dtype),
        in_specs=[pl.BlockSpec(memory_space=pltpu.SMEM), pl.BlockSpec(memory_space=pltpu.VMEM)],
        out_specs=pl.BlockSpec(memory_space=pltpu.VMEM),
        cost_estimate=pl.CostEstimate(flops=0, transcendentals=0, bytes_accessed=2 * side_by_side.size * 4),
    )(order, side_by_side)


def shards(noise, inv_diag, coupling, order):
    block_count = noise.shape[0]
    node_count = noise.shape[1]
    sample_count = noise.shape[2]
    coupling_full = line_all_gather(coupling, "cols")
    noise_rows = line_all_to_all(noise, "cols")
    partial = jnp.stack(
        [apply(split(inv_diag[block], 2), noise_rows[block]) for block in range(block_count)], axis=0
    )
    coupling_parts = [split(coupling_full[block], 2) for block in range(block_count)]
    across = coupling_full[block_count - 1]
    for block in range(block_count - 2, -1, -1):
        across = apply(coupling_parts[block], across)
    driven_all, across_parts = line_reduce_scatter(partial, "cols", split(across, 2))
    driven = [driven_all[block] for block in range(block_count)]

    def chain(entering, skip_last):
        carried = entering
        results = [None] * block_count
        for block in range(block_count - 1, -1, -1):
            if skip_last and block == block_count - 1:
                carried = driven[block]
            else:
                carried = driven[block] + apply(coupling_parts[block], carried)
            results[block] = carried
        return results

    local = chain(None, True)[0]
    relays = lax.axis_size("tm")
    entering = jnp.zeros_like(driven[0])
    for step in range(relays - 1):
        sender = relays - 1 - step
        leaving = local if step == 0 else local + apply(across_parts, entering)
        entering = entering + lax.ppermute(leaving, "tm", [(sender, sender - 1)])
    finals = chain(entering, False)
    return pick_rows(finals, order)


def solution(mesh):
    return jax.shard_map(
        shards,
        mesh=mesh,
        in_specs=(
            P(("parts", "tm"), None, "cols"),
            P(("parts", "tm"), None, "cols"),
            P(("parts", "tm"), None, "cols"),
            P(),
        ),
        out_specs=P(("parts", "tm"), None, "cols"),
        check_vma=False,
    )
```

```python
import jax
import jax.numpy as jnp
from jax import lax
from jax.sharding import PartitionSpec as P
from jax.experimental import pallas as pl
from jax.experimental.pallas import tpu as pltpu

low = jnp.bfloat16


def shifted(block, axis, distance):
    devices = range(lax.axis_size(axis))
    route = [(i - distance, i) for i in devices if i - distance in devices]
    return lax.ppermute(block, axis, route)


def split(value, count):
    parts = []
    rest = value
    for index in range(count):
        kept = lax.reduce_precision(rest, exponent_bits=8, mantissa_bits=7)
        parts.append(kept.astype(low))
        if index < count - 1:
            rest = rest - kept
    return parts


def bdot(left, right):
    return jnp.dot(left, right, preferred_element_type=jnp.float32)


def apply(matrix_parts, operand):
    high, small = matrix_parts
    width = operand.shape[1]
    operand_high, operand_small = split(operand, 2)
    both = bdot(high, jnp.concatenate([operand_high, operand_small], axis=1))
    return both[:, :width] + (both[:, width:] + bdot(small, operand_high))


def line_reduce_scatter(partial, axis, ready=None):
    count = lax.axis_size(axis)
    me = lax.axis_index(axis)
    width = partial.shape[2] // count

    def tile(owner):
        owner = jnp.clip(owner, 0, count - 1)
        return lax.dynamic_slice_in_dim(partial, owner * width, width, axis=2)

    rightward = jnp.zeros_like(tile(me))
    leftward = jnp.zeros_like(tile(me))
    for step in range(1, count):
        right_route = [(k, k + 1) for k in range(0, min(step, count - 1))]
        left_route = [(k, k - 1) for k in range(max(count - step, 1), count)]
        rightward = lax.ppermute(tile(me + count - step) + rightward, axis, right_route)
        leftward = lax.ppermute(tile(me - count + step) + leftward, axis, left_route)
    if ready is not None:
        rightward, leftward, ready = lax.optimization_barrier((rightward, leftward, ready))
    return tile(me) + (rightward + leftward), ready


def add_at(whole, piece, slot, axis):
    count = whole.shape[axis] // piece.shape[axis]
    start = jnp.clip(slot, 0, count - 1) * piece.shape[axis]
    current = lax.dynamic_slice_in_dim(whole, start, piece.shape[axis], axis=axis)
    return lax.dynamic_update_slice_in_dim(whole, current + piece, start, axis=axis)


def line_all_gather(tile, axis):
    count = lax.axis_size(axis)
    me = lax.axis_index(axis)
    last = tile.ndim - 1
    shape = tile.shape[:-1] + (count * tile.shape[-1],)
    whole = add_at(jnp.zeros(shape, tile.dtype), tile, me, last)
    from_left = tile
    from_right = tile
    for step in range(1, count):
        from_left = lax.ppermute(from_left, axis, [(k, k + 1) for k in range(step - 1, count - 1)])
        from_right = lax.ppermute(from_right, axis, [(k, k - 1) for k in range(1, count - step + 1)])
        whole = add_at(whole, from_left, me - step, last)
        whole = add_at(whole, from_right, me + step, last)
    return whole


def line_all_to_all(value, axis):
    count = lax.axis_size(axis)
    me = lax.axis_index(axis)
    rows = value.shape[1] // count

    def own_rows(target):
        return lax.dynamic_slice_in_dim(value, jnp.clip(target, 0, count - 1) * rows, rows, axis=1)

    shape = (value.shape[0], rows, count * value.shape[2])
    whole = add_at(jnp.zeros(shape, value.dtype), own_rows(me), me, 2)
    for distance in range(1, count):
        right = lax.ppermute(own_rows(me + distance), axis, [(k, k + distance) for k in range(0, count - distance)])
        left = lax.ppermute(own_rows(me - distance), axis, [(k, k - distance) for k in range(distance, count)])
        whole = add_at(whole, right, me - distance, 2)
        whole = add_at(whole, left, me + distance, 2)
    return whole


def pick_rows_kernel(order_ref, field_ref, out_ref):
    blocks = field_ref.shape[0]
    group = 8

    def body(index, carry):
        start = pl.multiple_of(index * group, group)
        sources = [order_ref[start + row] for row in range(group)]
        for block in range(blocks):
            rows = [field_ref[block, pl.ds(source, 1), :] for source in sources]
            out_ref[block, pl.ds(start, group), :] = jnp.concatenate(rows, axis=0)
        return carry

    lax.fori_loop(0, field_ref.shape[1] // group, body, 0, unroll=8)


def pick_rows(field, order):
    return pl.pallas_call(
        pick_rows_kernel,
        out_shape=jax.ShapeDtypeStruct(field.shape, field.dtype),
        in_specs=[pl.BlockSpec(memory_space=pltpu.SMEM), pl.BlockSpec(memory_space=pltpu.VMEM)],
        out_specs=pl.BlockSpec(memory_space=pltpu.VMEM),
        cost_estimate=pl.CostEstimate(flops=0, transcendentals=0, bytes_accessed=2 * field.size * 4),
    )(order, field)


def shards(noise, inv_diag, coupling, order):
    block_count = noise.shape[0]
    node_count = noise.shape[1]
    sample_count = noise.shape[2]
    coupling_full = line_all_gather(coupling, "cols")
    noise_rows = line_all_to_all(noise, "cols")
    partial = jnp.stack(
        [apply(split(inv_diag[block], 2), noise_rows[block]) for block in range(block_count)], axis=0
    )
    coupling_parts = [split(coupling_full[block], 2) for block in range(block_count)]
    across = coupling_full[block_count - 1]
    for block in range(block_count - 2, -1, -1):
        across = apply(coupling_parts[block], across)
    driven_all, across_parts = line_reduce_scatter(partial, "cols", split(across, 2))
    driven = [driven_all[block] for block in range(block_count)]

    def chain(entering, skip_last):
        carried = entering
        results = [None] * block_count
        for block in range(block_count - 1, -1, -1):
            if skip_last and block == block_count - 1:
                carried = driven[block]
            else:
                carried = driven[block] + apply(coupling_parts[block], carried)
            results[block] = carried
        return results

    local = chain(None, True)[0]
    relays = lax.axis_size("tm")
    entering = jnp.zeros_like(driven[0])
    for step in range(relays - 1):
        sender = relays - 1 - step
        leaving = local if step == 0 else local + apply(across_parts, entering)
        entering = entering + lax.ppermute(leaving, "tm", [(sender, sender - 1)])
    finals = chain(entering, False)
    return pick_rows(jnp.stack(finals, axis=0), order)


def solution(mesh):
    return jax.shard_map(
        shards,
        mesh=mesh,
        in_specs=(
            P(("parts", "tm"), None, "cols"),
            P(("parts", "tm"), None, "cols"),
            P(("parts", "tm"), None, "cols"),
            P(),
        ),
        out_specs=P(("parts", "tm"), None, "cols"),
        check_vma=False,
    )
```

```python
import jax
import jax.numpy as jnp
from jax import lax
from jax.sharding import PartitionSpec as P
from jax.experimental import pallas as pl
from jax.experimental.pallas import tpu as pltpu

low = jnp.bfloat16


def shifted(block, axis, distance):
    devices = range(lax.axis_size(axis))
    route = [(i - distance, i) for i in devices if i - distance in devices]
    return lax.ppermute(block, axis, route)


def split(value, count):
    parts = []
    rest = value
    for index in range(count):
        kept = lax.reduce_precision(rest, exponent_bits=8, mantissa_bits=7)
        parts.append(kept.astype(low))
        if index < count - 1:
            rest = rest - kept
    return parts


def bdot(left, right):
    return jnp.dot(left, right, preferred_element_type=jnp.float32)


def apply(matrix_parts, operand):
    high, small = matrix_parts
    width = operand.shape[1]
    operand_high, operand_small = split(operand, 2)
    both = bdot(high, jnp.concatenate([operand_high, operand_small], axis=1))
    return both[:, :width] + (both[:, width:] + bdot(small, operand_high))


def line_reduce_scatter(partial, axis, ready=None):
    count = lax.axis_size(axis)
    me = lax.axis_index(axis)
    width = partial.shape[2] // count

    def tile(owner):
        owner = jnp.clip(owner, 0, count - 1)
        return lax.dynamic_slice_in_dim(partial, owner * width, width, axis=2)

    rightward = jnp.zeros_like(tile(me))
    leftward = jnp.zeros_like(tile(me))
    for step in range(1, count):
        right_route = [(k, k + 1) for k in range(0, min(step, count - 1))]
        left_route = [(k, k - 1) for k in range(max(count - step, 1), count)]
        rightward = lax.ppermute(tile(me + count - step) + rightward, axis, right_route)
        leftward = lax.ppermute(tile(me - count + step) + leftward, axis, left_route)
    if ready is not None:
        rightward, leftward, ready = lax.optimization_barrier((rightward, leftward, ready))
    return tile(me) + (rightward + leftward), ready


def add_at(whole, piece, slot, axis):
    count = whole.shape[axis] // piece.shape[axis]
    start = jnp.clip(slot, 0, count - 1) * piece.shape[axis]
    current = lax.dynamic_slice_in_dim(whole, start, piece.shape[axis], axis=axis)
    return lax.dynamic_update_slice_in_dim(whole, current + piece, start, axis=axis)


def line_all_gather(tile, axis):
    count = lax.axis_size(axis)
    me = lax.axis_index(axis)
    last = tile.ndim - 1
    shape = tile.shape[:-1] + (count * tile.shape[-1],)
    whole = add_at(jnp.zeros(shape, tile.dtype), tile, me, last)
    from_left = tile
    from_right = tile
    for step in range(1, count):
        from_left = lax.ppermute(from_left, axis, [(k, k + 1) for k in range(step - 1, count - 1)])
        from_right = lax.ppermute(from_right, axis, [(k, k - 1) for k in range(1, count - step + 1)])
        whole = add_at(whole, from_left, me - step, last)
        whole = add_at(whole, from_right, me + step, last)
    return whole


def line_all_to_all(value, axis):
    count = lax.axis_size(axis)
    me = lax.axis_index(axis)
    rows = value.shape[1] // count

    def own_rows(target):
        return lax.dynamic_slice_in_dim(value, jnp.clip(target, 0, count - 1) * rows, rows, axis=1)

    shape = (value.shape[0], rows, count * value.shape[2])
    whole = add_at(jnp.zeros(shape, value.dtype), own_rows(me), me, 2)
    for distance in range(1, count):
        right = lax.ppermute(own_rows(me + distance), axis, [(k, k + distance) for k in range(0, count - distance)])
        left = lax.ppermute(own_rows(me - distance), axis, [(k, k - distance) for k in range(distance, count)])
        whole = add_at(whole, right, me - distance, 2)
        whole = add_at(whole, left, me + distance, 2)
    return whole


def pick_rows_kernel(order_ref, field_ref, out_ref):
    blocks = field_ref.shape[0]
    group = 8

    def body(index, carry):
        start = pl.multiple_of(index * group, group)
        sources = [order_ref[start + row] for row in range(group)]
        for block in range(blocks):
            rows = [field_ref[block, pl.ds(source, 1), :] for source in sources]
            out_ref[block, pl.ds(start, group), :] = jnp.concatenate(rows, axis=0)
        return carry

    lax.fori_loop(0, field_ref.shape[1] // group, body, 0, unroll=2)


def pick_rows(field, order):
    return pl.pallas_call(
        pick_rows_kernel,
        out_shape=jax.ShapeDtypeStruct(field.shape, field.dtype),
        in_specs=[pl.BlockSpec(memory_space=pltpu.SMEM), pl.BlockSpec(memory_space=pltpu.VMEM)],
        out_specs=pl.BlockSpec(memory_space=pltpu.VMEM),
        cost_estimate=pl.CostEstimate(flops=0, transcendentals=0, bytes_accessed=2 * field.size * 4),
    )(order, field)


def shards(noise, inv_diag, coupling, order):
    block_count = noise.shape[0]
    node_count = noise.shape[1]
    sample_count = noise.shape[2]
    coupling_full = line_all_gather(coupling, "cols")
    noise_rows = line_all_to_all(noise, "cols")
    partial = jnp.stack(
        [apply(split(inv_diag[block], 2), noise_rows[block]) for block in range(block_count)], axis=0
    )
    coupling_parts = [split(coupling_full[block], 2) for block in range(block_count)]
    across = coupling_full[block_count - 1]
    for block in range(block_count - 2, -1, -1):
        across = apply(coupling_parts[block], across)
    driven_all, across_parts = line_reduce_scatter(partial, "cols", split(across, 2))
    driven = [driven_all[block] for block in range(block_count)]

    def chain(entering, skip_last):
        carried = entering
        results = [None] * block_count
        for block in range(block_count - 1, -1, -1):
            if skip_last and block == block_count - 1:
                carried = driven[block]
            else:
                carried = driven[block] + apply(coupling_parts[block], carried)
            results[block] = carried
        return results

    local = chain(None, True)[0]
    relays = lax.axis_size("tm")
    entering = jnp.zeros_like(driven[0])
    for step in range(relays - 1):
        sender = relays - 1 - step
        leaving = local if step == 0 else local + apply(across_parts, entering)
        entering = entering + lax.ppermute(leaving, "tm", [(sender, sender - 1)])
    if block_count == 2:
        finals = [local + apply(across_parts, entering), driven[1] + apply(coupling_parts[1], entering)]
    else:
        finals = chain(entering, False)
    return pick_rows(jnp.stack(finals, axis=0), order)


def solution(mesh):
    return jax.shard_map(
        shards,
        mesh=mesh,
        in_specs=(
            P(("parts", "tm"), None, "cols"),
            P(("parts", "tm"), None, "cols"),
            P(("parts", "tm"), None, "cols"),
            P(),
        ),
        out_specs=P(("parts", "tm"), None, "cols"),
        check_vma=False,
    )
```

```python
import jax
import jax.numpy as jnp
from jax import lax
from jax.sharding import PartitionSpec as P
from jax.experimental import pallas as pl
from jax.experimental.pallas import tpu as pltpu

low = jnp.bfloat16


def shifted(block, axis, distance):
    devices = range(lax.axis_size(axis))
    route = [(i - distance, i) for i in devices if i - distance in devices]
    return lax.ppermute(block, axis, route)


def split(value, count):
    parts = []
    rest = value
    for index in range(count):
        kept = lax.reduce_precision(rest, exponent_bits=8, mantissa_bits=7)
        parts.append(kept.astype(low))
        if index < count - 1:
            rest = rest - kept
    return parts


def bdot(left, right):
    return jnp.dot(left, right, preferred_element_type=jnp.float32)


def apply(matrix_parts, operand):
    high, small = matrix_parts
    width = operand.shape[1]
    operand_high, operand_small = split(operand, 2)
    both = bdot(high, jnp.concatenate([operand_high, operand_small], axis=1))
    return both[:, :width] + (both[:, width:] + bdot(small, operand_high))


def line_reduce_scatter(partial, axis, ready=None):
    count = lax.axis_size(axis)
    me = lax.axis_index(axis)
    width = partial.shape[2] // count

    def tile(owner):
        owner = jnp.clip(owner, 0, count - 1)
        return lax.dynamic_slice_in_dim(partial, owner * width, width, axis=2)

    rightward = jnp.zeros_like(tile(me))
    leftward = jnp.zeros_like(tile(me))
    for step in range(1, count):
        right_route = [(k, k + 1) for k in range(0, min(step, count - 1))]
        left_route = [(k, k - 1) for k in range(max(count - step, 1), count)]
        rightward = lax.ppermute(tile(me + count - step) + rightward, axis, right_route)
        leftward = lax.ppermute(tile(me - count + step) + leftward, axis, left_route)
    if ready is not None:
        rightward, leftward, ready = lax.optimization_barrier((rightward, leftward, ready))
    return tile(me) + (rightward + leftward), ready


def add_at(whole, piece, slot, axis):
    count = whole.shape[axis] // piece.shape[axis]
    start = jnp.clip(slot, 0, count - 1) * piece.shape[axis]
    current = lax.dynamic_slice_in_dim(whole, start, piece.shape[axis], axis=axis)
    return lax.dynamic_update_slice_in_dim(whole, current + piece, start, axis=axis)


def line_all_gather(tile, axis):
    count = lax.axis_size(axis)
    me = lax.axis_index(axis)
    last = tile.ndim - 1
    shape = tile.shape[:-1] + (count * tile.shape[-1],)
    whole = add_at(jnp.zeros(shape, tile.dtype), tile, me, last)
    from_left = tile
    from_right = tile
    for step in range(1, count):
        from_left = lax.ppermute(from_left, axis, [(k, k + 1) for k in range(step - 1, count - 1)])
        from_right = lax.ppermute(from_right, axis, [(k, k - 1) for k in range(1, count - step + 1)])
        whole = add_at(whole, from_left, me - step, last)
        whole = add_at(whole, from_right, me + step, last)
    return whole


def line_all_to_all(value, axis):
    count = lax.axis_size(axis)
    me = lax.axis_index(axis)
    rows = value.shape[1] // count

    def own_rows(target):
        return lax.dynamic_slice_in_dim(value, jnp.clip(target, 0, count - 1) * rows, rows, axis=1)

    shape = (value.shape[0], rows, count * value.shape[2])
    whole = add_at(jnp.zeros(shape, value.dtype), own_rows(me), me, 2)
    for distance in range(1, count):
        right = lax.ppermute(own_rows(me + distance), axis, [(k, k + distance) for k in range(0, count - distance)])
        left = lax.ppermute(own_rows(me - distance), axis, [(k, k - distance) for k in range(distance, count)])
        whole = add_at(whole, right, me - distance, 2)
        whole = add_at(whole, left, me + distance, 2)
    return whole


def pick_rows_kernel(order_ref, field_ref, out_ref):
    blocks = field_ref.shape[0]
    group = 8

    def body(index, carry):
        start = pl.multiple_of(index * group, group)
        sources = [order_ref[start + row] for row in range(group)]
        for block in range(blocks):
            rows = [field_ref[block, pl.ds(source, 1), :] for source in sources]
            out_ref[block, pl.ds(start, group), :] = jnp.concatenate(rows, axis=0)
        return carry

    lax.fori_loop(0, field_ref.shape[1] // group, body, 0, unroll=2)


def pick_rows(field, order):
    return pl.pallas_call(
        pick_rows_kernel,
        out_shape=jax.ShapeDtypeStruct(field.shape, field.dtype),
        in_specs=[pl.BlockSpec(memory_space=pltpu.SMEM), pl.BlockSpec(memory_space=pltpu.VMEM)],
        out_specs=pl.BlockSpec(memory_space=pltpu.VMEM),
        cost_estimate=pl.CostEstimate(flops=0, transcendentals=0, bytes_accessed=2 * field.size * 4),
    )(order, field)


def shards(noise, inv_diag, coupling, order):
    block_count = noise.shape[0]
    node_count = noise.shape[1]
    sample_count = noise.shape[2]
    coupling_full = line_all_gather(coupling, "cols")
    noise_rows = line_all_to_all(noise, "cols")
    partial = jnp.stack(
        [apply(split(inv_diag[block], 2), noise_rows[block]) for block in range(block_count)], axis=0
    )
    coupling_parts = [split(coupling_full[block], 2) for block in range(block_count)]
    across = coupling_full[block_count - 1]
    for block in range(block_count - 2, -1, -1):
        across = apply(coupling_parts[block], across)
    if block_count == 2:
        picked_maps = pick_rows(jnp.stack([across, coupling_full[1]], axis=0), order)
        ready = (split(across, 2), split(picked_maps[0], 2), split(picked_maps[1], 2))
        driven_all, (across_parts, picked_across, picked_last) = line_reduce_scatter(partial, "cols", ready)
    else:
        driven_all, across_parts = line_reduce_scatter(partial, "cols", split(across, 2))
    driven = [driven_all[block] for block in range(block_count)]

    def chain(entering, skip_last):
        carried = entering
        results = [None] * block_count
        for block in range(block_count - 1, -1, -1):
            if skip_last and block == block_count - 1:
                carried = driven[block]
            else:
                carried = driven[block] + apply(coupling_parts[block], carried)
            results[block] = carried
        return results

    local = chain(None, True)[0]
    relays = lax.axis_size("tm")
    entering = jnp.zeros_like(driven[0])
    for step in range(relays - 1):
        sender = relays - 1 - step
        leaving = local if step == 0 else local + apply(across_parts, entering)
        entering = entering + lax.ppermute(leaving, "tm", [(sender, sender - 1)])
    if block_count == 2:
        picked_vectors = pick_rows(jnp.stack([local, driven[1]], axis=0), order)
        first_block = picked_vectors[0] + apply(picked_across, entering)
        last_block = picked_vectors[1] + apply(picked_last, entering)
        return jnp.stack([first_block, last_block], axis=0)
    finals = chain(entering, False)
    return pick_rows(jnp.stack(finals, axis=0), order)


def solution(mesh):
    return jax.shard_map(
        shards,
        mesh=mesh,
        in_specs=(
            P(("parts", "tm"), None, "cols"),
            P(("parts", "tm"), None, "cols"),
            P(("parts", "tm"), None, "cols"),
            P(),
        ),
        out_specs=P(("parts", "tm"), None, "cols"),
        check_vma=False,
    )
```

```python
import jax
import jax.numpy as jnp
from jax import lax
from jax.sharding import PartitionSpec as P
from jax.experimental import pallas as pl
from jax.experimental.pallas import tpu as pltpu

low = jnp.bfloat16


def shifted(block, axis, distance):
    devices = range(lax.axis_size(axis))
    route = [(i - distance, i) for i in devices if i - distance in devices]
    return lax.ppermute(block, axis, route)


def split(value, count):
    parts = []
    rest = value
    for index in range(count):
        kept = lax.reduce_precision(rest, exponent_bits=8, mantissa_bits=7)
        parts.append(kept.astype(low))
        if index < count - 1:
            rest = rest - kept
    return parts


def bdot(left, right):
    return jnp.dot(left, right, preferred_element_type=jnp.float32)


def apply(matrix_parts, operand):
    high, small = matrix_parts
    width = operand.shape[1]
    operand_high, operand_small = split(operand, 2)
    both = bdot(high, jnp.concatenate([operand_high, operand_small], axis=1))
    return both[:, :width] + (both[:, width:] + bdot(small, operand_high))


def line_reduce_scatter(partial, axis, ready=None):
    count = lax.axis_size(axis)
    me = lax.axis_index(axis)
    width = partial.shape[2] // count

    def tile(owner):
        owner = jnp.clip(owner, 0, count - 1)
        return lax.dynamic_slice_in_dim(partial, owner * width, width, axis=2)

    rightward = jnp.zeros_like(tile(me))
    leftward = jnp.zeros_like(tile(me))
    for step in range(1, count):
        right_route = [(k, k + 1) for k in range(0, min(step, count - 1))]
        left_route = [(k, k - 1) for k in range(max(count - step, 1), count)]
        rightward = lax.ppermute(tile(me + count - step) + rightward, axis, right_route)
        leftward = lax.ppermute(tile(me - count + step) + leftward, axis, left_route)
    if ready is not None:
        rightward, leftward, ready = lax.optimization_barrier((rightward, leftward, ready))
    return tile(me) + (rightward + leftward), ready


def add_at(whole, piece, slot, axis):
    count = whole.shape[axis] // piece.shape[axis]
    start = jnp.clip(slot, 0, count - 1) * piece.shape[axis]
    current = lax.dynamic_slice_in_dim(whole, start, piece.shape[axis], axis=axis)
    return lax.dynamic_update_slice_in_dim(whole, current + piece, start, axis=axis)


def line_all_gather(tile, axis):
    count = lax.axis_size(axis)
    me = lax.axis_index(axis)
    last = tile.ndim - 1
    shape = tile.shape[:-1] + (count * tile.shape[-1],)
    whole = add_at(jnp.zeros(shape, tile.dtype), tile, me, last)
    from_left = tile
    from_right = tile
    for step in range(1, count):
        from_left = lax.ppermute(from_left, axis, [(k, k + 1) for k in range(step - 1, count - 1)])
        from_right = lax.ppermute(from_right, axis, [(k, k - 1) for k in range(1, count - step + 1)])
        whole = add_at(whole, from_left, me - step, last)
        whole = add_at(whole, from_right, me + step, last)
    return whole


def line_all_to_all(value, axis):
    count = lax.axis_size(axis)
    me = lax.axis_index(axis)
    rows = value.shape[1] // count

    def own_rows(target):
        return lax.dynamic_slice_in_dim(value, jnp.clip(target, 0, count - 1) * rows, rows, axis=1)

    shape = (value.shape[0], rows, count * value.shape[2])
    whole = add_at(jnp.zeros(shape, value.dtype), own_rows(me), me, 2)
    for distance in range(1, count):
        right = lax.ppermute(own_rows(me + distance), axis, [(k, k + distance) for k in range(0, count - distance)])
        left = lax.ppermute(own_rows(me - distance), axis, [(k, k - distance) for k in range(distance, count)])
        whole = add_at(whole, right, me - distance, 2)
        whole = add_at(whole, left, me + distance, 2)
    return whole


def pick_rows_kernel(order_ref, field_ref, out_ref):
    blocks = field_ref.shape[0]
    group = 16

    def body(index, carry):
        start = pl.multiple_of(index * group, group)
        sources = [order_ref[start + row] for row in range(group)]
        for block in range(blocks):
            rows = [field_ref[block, pl.ds(source, 1), :] for source in sources]
            out_ref[block, pl.ds(start, group), :] = jnp.concatenate(rows, axis=0)
        return carry

    lax.fori_loop(0, field_ref.shape[1] // group, body, 0, unroll=2)


def pick_rows(field, order):
    return pl.pallas_call(
        pick_rows_kernel,
        out_shape=jax.ShapeDtypeStruct(field.shape, field.dtype),
        in_specs=[pl.BlockSpec(memory_space=pltpu.SMEM), pl.BlockSpec(memory_space=pltpu.VMEM)],
        out_specs=pl.BlockSpec(memory_space=pltpu.VMEM),
        cost_estimate=pl.CostEstimate(flops=0, transcendentals=0, bytes_accessed=2 * field.size * 4),
    )(order, field)


def shards(noise, inv_diag, coupling, order):
    block_count = noise.shape[0]
    node_count = noise.shape[1]
    sample_count = noise.shape[2]
    coupling_full = line_all_gather(coupling, "cols")
    noise_rows = line_all_to_all(noise, "cols")
    partial = jnp.stack(
        [apply(split(inv_diag[block], 2), noise_rows[block]) for block in range(block_count)], axis=0
    )
    coupling_parts = [split(coupling_full[block], 2) for block in range(block_count)]
    across = coupling_full[block_count - 1]
    for block in range(block_count - 2, -1, -1):
        across = apply(coupling_parts[block], across)
    driven_all, across_parts = line_reduce_scatter(partial, "cols", split(across, 2))
    driven = [driven_all[block] for block in range(block_count)]

    def chain(entering, skip_last):
        carried = entering
        results = [None] * block_count
        for block in range(block_count - 1, -1, -1):
            if skip_last and block == block_count - 1:
                carried = driven[block]
            else:
                carried = driven[block] + apply(coupling_parts[block], carried)
            results[block] = carried
        return results

    local = chain(None, True)[0]
    relays = lax.axis_size("tm")
    entering = jnp.zeros_like(driven[0])
    for step in range(relays - 1):
        sender = relays - 1 - step
        leaving = local if step == 0 else local + apply(across_parts, entering)
        entering = entering + lax.ppermute(leaving, "tm", [(sender, sender - 1)])
    if block_count == 2:
        finals = [local + apply(across_parts, entering), driven[1] + apply(coupling_parts[1], entering)]
    else:
        finals = chain(entering, False)
    return pick_rows(jnp.stack(finals, axis=0), order)


def solution(mesh):
    return jax.shard_map(
        shards,
        mesh=mesh,
        in_specs=(
            P(("parts", "tm"), None, "cols"),
            P(("parts", "tm"), None, "cols"),
            P(("parts", "tm"), None, "cols"),
            P(),
        ),
        out_specs=P(("parts", "tm"), None, "cols"),
        check_vma=False,
    )
```

```python
import jax
import jax.numpy as jnp
from jax import lax
from jax.sharding import PartitionSpec as P
from jax.experimental import pallas as pl
from jax.experimental.pallas import tpu as pltpu

low = jnp.bfloat16


def shifted(block, axis, distance):
    devices = range(lax.axis_size(axis))
    route = [(i - distance, i) for i in devices if i - distance in devices]
    return lax.ppermute(block, axis, route)


def split(value, count):
    parts = []
    rest = value
    for index in range(count):
        kept = lax.reduce_precision(rest, exponent_bits=8, mantissa_bits=7)
        parts.append(kept.astype(low))
        if index < count - 1:
            rest = rest - kept
    return parts


def bdot(left, right):
    return jnp.dot(left, right, preferred_element_type=jnp.float32)


def apply(matrix_parts, operand):
    high, small = matrix_parts
    width = operand.shape[1]
    operand_high, operand_small = split(operand, 2)
    both = bdot(high, jnp.concatenate([operand_high, operand_small], axis=1))
    return both[:, :width] + (both[:, width:] + bdot(small, operand_high))


def line_reduce_scatter(partial, axis, ready=None):
    count = lax.axis_size(axis)
    me = lax.axis_index(axis)
    width = partial.shape[2] // count

    def tile(owner):
        owner = jnp.clip(owner, 0, count - 1)
        return lax.dynamic_slice_in_dim(partial, owner * width, width, axis=2)

    rightward = jnp.zeros_like(tile(me))
    leftward = jnp.zeros_like(tile(me))
    for step in range(1, count):
        right_route = [(k, k + 1) for k in range(0, min(step, count - 1))]
        left_route = [(k, k - 1) for k in range(max(count - step, 1), count)]
        rightward = lax.ppermute(tile(me + count - step) + rightward, axis, right_route)
        leftward = lax.ppermute(tile(me - count + step) + leftward, axis, left_route)
    if ready is not None:
        rightward, leftward, ready = lax.optimization_barrier((rightward, leftward, ready))
    return tile(me) + (rightward + leftward), ready


def add_at(whole, piece, slot, axis):
    count = whole.shape[axis] // piece.shape[axis]
    start = jnp.clip(slot, 0, count - 1) * piece.shape[axis]
    current = lax.dynamic_slice_in_dim(whole, start, piece.shape[axis], axis=axis)
    return lax.dynamic_update_slice_in_dim(whole, current + piece, start, axis=axis)


def line_all_gather(tile, axis):
    count = lax.axis_size(axis)
    me = lax.axis_index(axis)
    last = tile.ndim - 1
    shape = tile.shape[:-1] + (count * tile.shape[-1],)
    whole = add_at(jnp.zeros(shape, tile.dtype), tile, me, last)
    from_left = tile
    from_right = tile
    for step in range(1, count):
        from_left = lax.ppermute(from_left, axis, [(k, k + 1) for k in range(step - 1, count - 1)])
        from_right = lax.ppermute(from_right, axis, [(k, k - 1) for k in range(1, count - step + 1)])
        whole = add_at(whole, from_left, me - step, last)
        whole = add_at(whole, from_right, me + step, last)
    return whole


def line_all_to_all(value, axis):
    count = lax.axis_size(axis)
    me = lax.axis_index(axis)
    rows = value.shape[1] // count

    def own_rows(target):
        return lax.dynamic_slice_in_dim(value, jnp.clip(target, 0, count - 1) * rows, rows, axis=1)

    shape = (value.shape[0], rows, count * value.shape[2])
    whole = add_at(jnp.zeros(shape, value.dtype), own_rows(me), me, 2)
    for distance in range(count - 1, 0, -1):
        right = lax.ppermute(own_rows(me + distance), axis, [(k, k + distance) for k in range(0, count - distance)])
        left = lax.ppermute(own_rows(me - distance), axis, [(k, k - distance) for k in range(distance, count)])
        whole = add_at(whole, right, me - distance, 2)
        whole = add_at(whole, left, me + distance, 2)
    return whole


def pick_rows_kernel(order_ref, field_ref, out_ref):
    blocks = field_ref.shape[0]
    group = 8

    def body(index, carry):
        start = pl.multiple_of(index * group, group)
        sources = [order_ref[start + row] for row in range(group)]
        for block in range(blocks):
            rows = [field_ref[block, pl.ds(source, 1), :] for source in sources]
            out_ref[block, pl.ds(start, group), :] = jnp.concatenate(rows, axis=0)
        return carry

    lax.fori_loop(0, field_ref.shape[1] // group, body, 0, unroll=2)


def pick_rows(field, order):
    return pl.pallas_call(
        pick_rows_kernel,
        out_shape=jax.ShapeDtypeStruct(field.shape, field.dtype),
        in_specs=[pl.BlockSpec(memory_space=pltpu.SMEM), pl.BlockSpec(memory_space=pltpu.VMEM)],
        out_specs=pl.BlockSpec(memory_space=pltpu.VMEM),
        cost_estimate=pl.CostEstimate(flops=0, transcendentals=0, bytes_accessed=2 * field.size * 4),
    )(order, field)


def shards(noise, inv_diag, coupling, order):
    block_count = noise.shape[0]
    node_count = noise.shape[1]
    sample_count = noise.shape[2]
    coupling_full = line_all_gather(coupling, "cols")
    noise_rows = line_all_to_all(noise, "cols")
    partial = jnp.stack(
        [apply(split(inv_diag[block], 2), noise_rows[block]) for block in range(block_count)], axis=0
    )
    coupling_parts = [split(coupling_full[block], 2) for block in range(block_count)]
    across = coupling_full[block_count - 1]
    for block in range(block_count - 2, -1, -1):
        across = apply(coupling_parts[block], across)
    driven_all, across_parts = line_reduce_scatter(partial, "cols", split(across, 2))
    driven = [driven_all[block] for block in range(block_count)]

    def chain(entering, skip_last):
        carried = entering
        results = [None] * block_count
        for block in range(block_count - 1, -1, -1):
            if skip_last and block == block_count - 1:
                carried = driven[block]
            else:
                carried = driven[block] + apply(coupling_parts[block], carried)
            results[block] = carried
        return results

    local = chain(None, True)[0]
    relays = lax.axis_size("tm")
    entering = jnp.zeros_like(driven[0])
    for step in range(relays - 1):
        sender = relays - 1 - step
        leaving = local if step == 0 else local + apply(across_parts, entering)
        entering = entering + lax.ppermute(leaving, "tm", [(sender, sender - 1)])
    if block_count == 2:
        finals = [local + apply(across_parts, entering), driven[1] + apply(coupling_parts[1], entering)]
    else:
        finals = chain(entering, False)
    return pick_rows(jnp.stack(finals, axis=0), order)


def solution(mesh):
    return jax.shard_map(
        shards,
        mesh=mesh,
        in_specs=(
            P(("parts", "tm"), None, "cols"),
            P(("parts", "tm"), None, "cols"),
            P(("parts", "tm"), None, "cols"),
            P(),
        ),
        out_specs=P(("parts", "tm"), None, "cols"),
        check_vma=False,
    )
```

```python
import jax
import jax.numpy as jnp
from jax import lax
from jax.sharding import PartitionSpec as P
from jax.experimental import pallas as pl
from jax.experimental.pallas import tpu as pltpu

low = jnp.bfloat16


def shifted(block, axis, distance):
    devices = range(lax.axis_size(axis))
    route = [(i - distance, i) for i in devices if i - distance in devices]
    return lax.ppermute(block, axis, route)


def split(value, count):
    parts = []
    rest = value
    for index in range(count):
        kept = lax.reduce_precision(rest, exponent_bits=8, mantissa_bits=7)
        parts.append(kept.astype(low))
        if index < count - 1:
            rest = rest - kept
    return parts


def bdot(left, right):
    return jnp.dot(left, right, preferred_element_type=jnp.float32)


def apply(matrix_parts, operand):
    high, small = matrix_parts
    width = operand.shape[1]
    operand_high, operand_small = split(operand, 2)
    both = bdot(high, jnp.concatenate([operand_high, operand_small], axis=1))
    return both[:, :width] + (both[:, width:] + bdot(small, operand_high))


def line_reduce_scatter(partial, axis, ready=None):
    count = lax.axis_size(axis)
    me = lax.axis_index(axis)
    width = partial.shape[2] // count

    def tile(owner):
        owner = jnp.clip(owner, 0, count - 1)
        return lax.dynamic_slice_in_dim(partial, owner * width, width, axis=2)

    rightward = jnp.zeros_like(tile(me))
    leftward = jnp.zeros_like(tile(me))
    going_right = [tile(me + count - step) for step in range(1, count)]
    going_left = [tile(me - count + step) for step in range(1, count)]
    going_right, going_left = lax.optimization_barrier((going_right, going_left))
    for step in range(1, count):
        right_route = [(k, k + 1) for k in range(0, min(step, count - 1))]
        left_route = [(k, k - 1) for k in range(max(count - step, 1), count)]
        rightward = lax.ppermute(going_right[step - 1] + rightward, axis, right_route)
        leftward = lax.ppermute(going_left[step - 1] + leftward, axis, left_route)
    if ready is not None:
        rightward, leftward, ready = lax.optimization_barrier((rightward, leftward, ready))
    return tile(me) + (rightward + leftward), ready


def add_at(whole, piece, slot, axis):
    count = whole.shape[axis] // piece.shape[axis]
    start = jnp.clip(slot, 0, count - 1) * piece.shape[axis]
    current = lax.dynamic_slice_in_dim(whole, start, piece.shape[axis], axis=axis)
    return lax.dynamic_update_slice_in_dim(whole, current + piece, start, axis=axis)


def line_all_gather(tile, axis):
    count = lax.axis_size(axis)
    me = lax.axis_index(axis)
    last = tile.ndim - 1
    shape = tile.shape[:-1] + (count * tile.shape[-1],)
    whole = add_at(jnp.zeros(shape, tile.dtype), tile, me, last)
    from_left = tile
    from_right = tile
    for step in range(1, count):
        from_left = lax.ppermute(from_left, axis, [(k, k + 1) for k in range(step - 1, count - 1)])
        from_right = lax.ppermute(from_right, axis, [(k, k - 1) for k in range(1, count - step + 1)])
        whole = add_at(whole, from_left, me - step, last)
        whole = add_at(whole, from_right, me + step, last)
    return whole


def line_all_to_all(value, axis):
    count = lax.axis_size(axis)
    me = lax.axis_index(axis)
    rows = value.shape[1] // count

    def own_rows(target):
        return lax.dynamic_slice_in_dim(value, jnp.clip(target, 0, count - 1) * rows, rows, axis=1)

    shape = (value.shape[0], rows, count * value.shape[2])
    whole = add_at(jnp.zeros(shape, value.dtype), own_rows(me), me, 2)
    for distance in range(1, count):
        right = lax.ppermute(own_rows(me + distance), axis, [(k, k + distance) for k in range(0, count - distance)])
        left = lax.ppermute(own_rows(me - distance), axis, [(k, k - distance) for k in range(distance, count)])
        whole = add_at(whole, right, me - distance, 2)
        whole = add_at(whole, left, me + distance, 2)
    return whole


def pick_rows_kernel(order_ref, field_ref, out_ref):
    blocks = field_ref.shape[0]
    group = 8

    def body(index, carry):
        start = pl.multiple_of(index * group, group)
        sources = [order_ref[start + row] for row in range(group)]
        for block in range(blocks):
            rows = [field_ref[block, pl.ds(source, 1), :] for source in sources]
            out_ref[block, pl.ds(start, group), :] = jnp.concatenate(rows, axis=0)
        return carry

    lax.fori_loop(0, field_ref.shape[1] // group, body, 0, unroll=2)


def pick_rows(field, order):
    return pl.pallas_call(
        pick_rows_kernel,
        out_shape=jax.ShapeDtypeStruct(field.shape, field.dtype),
        in_specs=[pl.BlockSpec(memory_space=pltpu.SMEM), pl.BlockSpec(memory_space=pltpu.VMEM)],
        out_specs=pl.BlockSpec(memory_space=pltpu.VMEM),
        cost_estimate=pl.CostEstimate(flops=0, transcendentals=0, bytes_accessed=2 * field.size * 4),
    )(order, field)


def shards(noise, inv_diag, coupling, order):
    block_count = noise.shape[0]
    node_count = noise.shape[1]
    sample_count = noise.shape[2]
    coupling_full = line_all_gather(coupling, "cols")
    noise_rows = line_all_to_all(noise, "cols")
    partial = jnp.stack(
        [apply(split(inv_diag[block], 2), noise_rows[block]) for block in range(block_count)], axis=0
    )
    coupling_parts = [split(coupling_full[block], 2) for block in range(block_count)]
    across = coupling_full[block_count - 1]
    for block in range(block_count - 2, -1, -1):
        across = apply(coupling_parts[block], across)
    driven_all, across_parts = line_reduce_scatter(partial, "cols", split(across, 2))
    driven = [driven_all[block] for block in range(block_count)]

    def chain(entering, skip_last):
        carried = entering
        results = [None] * block_count
        for block in range(block_count - 1, -1, -1):
            if skip_last and block == block_count - 1:
                carried = driven[block]
            else:
                carried = driven[block] + apply(coupling_parts[block], carried)
            results[block] = carried
        return results

    local = chain(None, True)[0]
    relays = lax.axis_size("tm")
    entering = jnp.zeros_like(driven[0])
    for step in range(relays - 1):
        sender = relays - 1 - step
        leaving = local if step == 0 else local + apply(across_parts, entering)
        entering = entering + lax.ppermute(leaving, "tm", [(sender, sender - 1)])
    if block_count == 2:
        finals = [local + apply(across_parts, entering), driven[1] + apply(coupling_parts[1], entering)]
    else:
        finals = chain(entering, False)
    return pick_rows(jnp.stack(finals, axis=0), order)


def solution(mesh):
    return jax.shard_map(
        shards,
        mesh=mesh,
        in_specs=(
            P(("parts", "tm"), None, "cols"),
            P(("parts", "tm"), None, "cols"),
            P(("parts", "tm"), None, "cols"),
            P(),
        ),
        out_specs=P(("parts", "tm"), None, "cols"),
        check_vma=False,
    )
```

```python
import jax
import jax.numpy as jnp
from jax import lax
from jax.sharding import PartitionSpec as P
from jax.experimental import pallas as pl
from jax.experimental.pallas import tpu as pltpu

low = jnp.bfloat16


def shifted(block, axis, distance):
    devices = range(lax.axis_size(axis))
    route = [(i - distance, i) for i in devices if i - distance in devices]
    return lax.ppermute(block, axis, route)


def split(value, count):
    parts = []
    rest = value
    for index in range(count):
        kept = lax.reduce_precision(rest, exponent_bits=8, mantissa_bits=7)
        parts.append(kept.astype(low))
        if index < count - 1:
            rest = rest - kept
    return parts


def bdot(left, right):
    return jnp.dot(left, right, preferred_element_type=jnp.float32)


def apply(matrix_parts, operand):
    high, small = matrix_parts
    width = operand.shape[1]
    operand_high, operand_small = split(operand, 2)
    both = bdot(high, jnp.concatenate([operand_high, operand_small], axis=1))
    return both[:, :width] + (both[:, width:] + bdot(small, operand_high))


def line_reduce_scatter(partial, axis, ready=None):
    count = lax.axis_size(axis)
    me = lax.axis_index(axis)
    width = partial.shape[2] // count

    def tile(owner):
        owner = jnp.clip(owner, 0, count - 1)
        return lax.dynamic_slice_in_dim(partial, owner * width, width, axis=2)

    rightward = jnp.zeros_like(tile(me))
    leftward = jnp.zeros_like(tile(me))
    going_right = [tile(me + count - step) for step in range(1, count)]
    going_left = [tile(me - count + step) for step in range(1, count)]
    own_tile = tile(me)
    going_right, going_left, own_tile = lax.optimization_barrier((going_right, going_left, own_tile))
    for step in range(1, count):
        right_route = [(k, k + 1) for k in range(0, min(step, count - 1))]
        left_route = [(k, k - 1) for k in range(max(count - step, 1), count)]
        rightward = lax.ppermute(going_right[step - 1] + rightward, axis, right_route)
        leftward = lax.ppermute(going_left[step - 1] + leftward, axis, left_route)
    if ready is not None:
        rightward, leftward, ready = lax.optimization_barrier((rightward, leftward, ready))
    return own_tile + (rightward + leftward), ready


def add_at(whole, piece, slot, axis):
    count = whole.shape[axis] // piece.shape[axis]
    start = jnp.clip(slot, 0, count - 1) * piece.shape[axis]
    current = lax.dynamic_slice_in_dim(whole, start, piece.shape[axis], axis=axis)
    return lax.dynamic_update_slice_in_dim(whole, current + piece, start, axis=axis)


def line_all_gather(tile, axis):
    count = lax.axis_size(axis)
    me = lax.axis_index(axis)
    last = tile.ndim - 1
    shape = tile.shape[:-1] + (count * tile.shape[-1],)
    whole = add_at(jnp.zeros(shape, tile.dtype), tile, me, last)
    from_left = tile
    from_right = tile
    for step in range(1, count):
        from_left = lax.ppermute(from_left, axis, [(k, k + 1) for k in range(step - 1, count - 1)])
        from_right = lax.ppermute(from_right, axis, [(k, k - 1) for k in range(1, count - step + 1)])
        whole = add_at(whole, from_left, me - step, last)
        whole = add_at(whole, from_right, me + step, last)
    return whole


def line_all_to_all(value, axis):
    count = lax.axis_size(axis)
    me = lax.axis_index(axis)
    rows = value.shape[1] // count

    def own_rows(target):
        return lax.dynamic_slice_in_dim(value, jnp.clip(target, 0, count - 1) * rows, rows, axis=1)

    shape = (value.shape[0], rows, count * value.shape[2])
    whole = add_at(jnp.zeros(shape, value.dtype), own_rows(me), me, 2)
    for distance in range(1, count):
        right = lax.ppermute(own_rows(me + distance), axis, [(k, k + distance) for k in range(0, count - distance)])
        left = lax.ppermute(own_rows(me - distance), axis, [(k, k - distance) for k in range(distance, count)])
        whole = add_at(whole, right, me - distance, 2)
        whole = add_at(whole, left, me + distance, 2)
    return whole


def pick_rows_kernel(order_ref, field_ref, out_ref):
    blocks = field_ref.shape[0]
    group = 8

    def body(index, carry):
        start = pl.multiple_of(index * group, group)
        sources = [order_ref[start + row] for row in range(group)]
        for block in range(blocks):
            rows = [field_ref[block, pl.ds(source, 1), :] for source in sources]
            out_ref[block, pl.ds(start, group), :] = jnp.concatenate(rows, axis=0)
        return carry

    lax.fori_loop(0, field_ref.shape[1] // group, body, 0, unroll=2)


def pick_rows(field, order):
    return pl.pallas_call(
        pick_rows_kernel,
        out_shape=jax.ShapeDtypeStruct(field.shape, field.dtype),
        in_specs=[pl.BlockSpec(memory_space=pltpu.SMEM), pl.BlockSpec(memory_space=pltpu.VMEM)],
        out_specs=pl.BlockSpec(memory_space=pltpu.VMEM),
        cost_estimate=pl.CostEstimate(flops=0, transcendentals=0, bytes_accessed=2 * field.size * 4),
    )(order, field)


def shards(noise, inv_diag, coupling, order):
    block_count = noise.shape[0]
    node_count = noise.shape[1]
    sample_count = noise.shape[2]
    coupling_full = line_all_gather(coupling, "cols")
    noise_rows = line_all_to_all(noise, "cols")
    partial = jnp.stack(
        [apply(split(inv_diag[block], 2), noise_rows[block]) for block in range(block_count)], axis=0
    )
    coupling_parts = [split(coupling_full[block], 2) for block in range(block_count)]
    across = coupling_full[block_count - 1]
    for block in range(block_count - 2, -1, -1):
        across = apply(coupling_parts[block], across)
    driven_all, across_parts = line_reduce_scatter(partial, "cols", split(across, 2))
    driven = [driven_all[block] for block in range(block_count)]

    def chain(entering, skip_last):
        carried = entering
        results = [None] * block_count
        for block in range(block_count - 1, -1, -1):
            if skip_last and block == block_count - 1:
                carried = driven[block]
            else:
                carried = driven[block] + apply(coupling_parts[block], carried)
            results[block] = carried
        return results

    local = chain(None, True)[0]
    relays = lax.axis_size("tm")
    entering = jnp.zeros_like(driven[0])
    for step in range(relays - 1):
        sender = relays - 1 - step
        leaving = local if step == 0 else local + apply(across_parts, entering)
        entering = entering + lax.ppermute(leaving, "tm", [(sender, sender - 1)])
    if block_count == 2:
        finals = [local + apply(across_parts, entering), driven[1] + apply(coupling_parts[1], entering)]
    else:
        finals = chain(entering, False)
    return pick_rows(jnp.stack(finals, axis=0), order)


def solution(mesh):
    return jax.shard_map(
        shards,
        mesh=mesh,
        in_specs=(
            P(("parts", "tm"), None, "cols"),
            P(("parts", "tm"), None, "cols"),
            P(("parts", "tm"), None, "cols"),
            P(),
        ),
        out_specs=P(("parts", "tm"), None, "cols"),
        check_vma=False,
    )
```

```python
import jax
import jax.numpy as jnp
from jax import lax
from jax.sharding import PartitionSpec as P
from jax.experimental import pallas as pl
from jax.experimental.pallas import tpu as pltpu

low = jnp.bfloat16


def shifted(block, axis, distance):
    devices = range(lax.axis_size(axis))
    route = [(i - distance, i) for i in devices if i - distance in devices]
    return lax.ppermute(block, axis, route)


def split(value, count):
    parts = []
    rest = value
    for index in range(count):
        kept = lax.reduce_precision(rest, exponent_bits=8, mantissa_bits=7)
        parts.append(kept.astype(low))
        if index < count - 1:
            rest = rest - kept
    return parts


def bdot(left, right):
    return jnp.dot(left, right, preferred_element_type=jnp.float32)


def apply(matrix_parts, operand):
    high, small = matrix_parts
    width = operand.shape[1]
    operand_high, operand_small = split(operand, 2)
    both = bdot(high, jnp.concatenate([operand_high, operand_small], axis=1))
    return both[:, :width] + (both[:, width:] + bdot(small, operand_high))


def line_reduce_scatter(partial, axis, ready=None):
    count = lax.axis_size(axis)
    me = lax.axis_index(axis)
    width = partial.shape[2] // count

    def tile(owner):
        owner = jnp.clip(owner, 0, count - 1)
        return lax.dynamic_slice_in_dim(partial, owner * width, width, axis=2)

    rightward = jnp.zeros_like(tile(me))
    leftward = jnp.zeros_like(tile(me))
    going_right = [tile(me + count - step) for step in range(1, count)]
    going_left = [tile(me - count + step) for step in range(1, count)]
    own_tile = tile(me)
    going_right, going_left, own_tile = lax.optimization_barrier((going_right, going_left, own_tile))
    for step in range(1, count):
        right_route = [(k, k + 1) for k in range(0, min(step, count - 1))]
        left_route = [(k, k - 1) for k in range(max(count - step, 1), count)]
        rightward = lax.ppermute(going_right[step - 1] + rightward, axis, right_route)
        leftward = lax.ppermute(going_left[step - 1] + leftward, axis, left_route)
    if ready is not None:
        rightward, leftward, ready = lax.optimization_barrier((rightward, leftward, ready))
    return own_tile + (rightward + leftward), ready


def add_at(whole, piece, slot, axis):
    count = whole.shape[axis] // piece.shape[axis]
    start = jnp.clip(slot, 0, count - 1) * piece.shape[axis]
    current = lax.dynamic_slice_in_dim(whole, start, piece.shape[axis], axis=axis)
    return lax.dynamic_update_slice_in_dim(whole, current + piece, start, axis=axis)


def line_all_gather(tile, axis):
    count = lax.axis_size(axis)
    me = lax.axis_index(axis)
    last = tile.ndim - 1
    shape = tile.shape[:-1] + (count * tile.shape[-1],)
    whole = add_at(jnp.zeros(shape, tile.dtype), tile, me, last)
    from_left = tile
    from_right = tile
    for step in range(1, count):
        from_left = lax.ppermute(from_left, axis, [(k, k + 1) for k in range(step - 1, count - 1)])
        from_right = lax.ppermute(from_right, axis, [(k, k - 1) for k in range(1, count - step + 1)])
        whole = add_at(whole, from_left, me - step, last)
        whole = add_at(whole, from_right, me + step, last)
    return whole


def line_all_to_all(value, axis):
    count = lax.axis_size(axis)
    me = lax.axis_index(axis)
    rows = value.shape[1] // count

    def own_rows(target):
        return lax.dynamic_slice_in_dim(value, jnp.clip(target, 0, count - 1) * rows, rows, axis=1)

    shape = (value.shape[0], rows, count * value.shape[2])
    whole = add_at(jnp.zeros(shape, value.dtype), own_rows(me), me, 2)
    sending = lax.optimization_barrier(
        [(own_rows(me + distance), own_rows(me - distance)) for distance in range(1, count)]
    )
    for distance in range(1, count):
        right = lax.ppermute(sending[distance - 1][0], axis, [(k, k + distance) for k in range(0, count - distance)])
        left = lax.ppermute(sending[distance - 1][1], axis, [(k, k - distance) for k in range(distance, count)])
        whole = add_at(whole, right, me - distance, 2)
        whole = add_at(whole, left, me + distance, 2)
    return whole


def pick_rows_kernel(order_ref, field_ref, out_ref):
    blocks = field_ref.shape[0]
    group = 8

    def body(index, carry):
        start = pl.multiple_of(index * group, group)
        sources = [order_ref[start + row] for row in range(group)]
        for block in range(blocks):
            rows = [field_ref[block, pl.ds(source, 1), :] for source in sources]
            out_ref[block, pl.ds(start, group), :] = jnp.concatenate(rows, axis=0)
        return carry

    lax.fori_loop(0, field_ref.shape[1] // group, body, 0, unroll=2)


def pick_rows(field, order):
    return pl.pallas_call(
        pick_rows_kernel,
        out_shape=jax.ShapeDtypeStruct(field.shape, field.dtype),
        in_specs=[pl.BlockSpec(memory_space=pltpu.SMEM), pl.BlockSpec(memory_space=pltpu.VMEM)],
        out_specs=pl.BlockSpec(memory_space=pltpu.VMEM),
        cost_estimate=pl.CostEstimate(flops=0, transcendentals=0, bytes_accessed=2 * field.size * 4),
    )(order, field)


def shards(noise, inv_diag, coupling, order):
    block_count = noise.shape[0]
    node_count = noise.shape[1]
    sample_count = noise.shape[2]
    coupling_full = line_all_gather(coupling, "cols")
    noise_rows = line_all_to_all(noise, "cols")
    partial = jnp.stack(
        [apply(split(inv_diag[block], 2), noise_rows[block]) for block in range(block_count)], axis=0
    )
    coupling_parts = [split(coupling_full[block], 2) for block in range(block_count)]
    across = coupling_full[block_count - 1]
    for block in range(block_count - 2, -1, -1):
        across = apply(coupling_parts[block], across)
    driven_all, across_parts = line_reduce_scatter(partial, "cols", split(across, 2))
    driven = [driven_all[block] for block in range(block_count)]

    def chain(entering, skip_last):
        carried = entering
        results = [None] * block_count
        for block in range(block_count - 1, -1, -1):
            if skip_last and block == block_count - 1:
                carried = driven[block]
            else:
                carried = driven[block] + apply(coupling_parts[block], carried)
            results[block] = carried
        return results

    local = chain(None, True)[0]
    relays = lax.axis_size("tm")
    entering = jnp.zeros_like(driven[0])
    for step in range(relays - 1):
        sender = relays - 1 - step
        leaving = local if step == 0 else local + apply(across_parts, entering)
        entering = entering + lax.ppermute(leaving, "tm", [(sender, sender - 1)])
    if block_count == 2:
        finals = [local + apply(across_parts, entering), driven[1] + apply(coupling_parts[1], entering)]
    else:
        finals = chain(entering, False)
    return pick_rows(jnp.stack(finals, axis=0), order)


def solution(mesh):
    return jax.shard_map(
        shards,
        mesh=mesh,
        in_specs=(
            P(("parts", "tm"), None, "cols"),
            P(("parts", "tm"), None, "cols"),
            P(("parts", "tm"), None, "cols"),
            P(),
        ),
        out_specs=P(("parts", "tm"), None, "cols"),
        check_vma=False,
    )
```
